256 devices in a mesh: req: 32 (over y, z_lo, core), tp: 8 (over x, z_hi).
Axes of the slice: x: 4, y: 4, z: 8 (z_hi: 2, z_lo: 4; z = z_hi * 4 + z_lo), core: 2. Of those that a mesh axis runs over, the one named last changes fastest.
Arguments:
- hidden_in: bfloat16 [8192, 2048], P('req', 'tp'), may hold values from -6 to 6
- embeds: bfloat16 [8192, 2048], P('req', 'tp'), may hold values from -6 to 6
- seg_ids: int32 [8192], replicated, may hold values from 0 to 15, never falling along the last dimension, each value on 1 to 2048 neighbouring positions
- mamba_gain: float32 [2048], replicated, may hold values from 0.5 to 1.5
- w_z: bfloat16 [2048, 2048], P(None, 'tp'), may hold values from -0.125 to 0.125
- w_x: bfloat16 [2048, 2048], P(None, 'tp'), may hold values from -0.125 to 0.125
- w_bc: bfloat16 [2048, 256], P('tp'), may hold values from -0.125 to 0.125
- w_dt: bfloat16 [2048, 32], P(None, 'tp'), may hold values from -0.125 to 0.125
- dt_bias: float32 [32], P('tp'), may hold values from -2 to 0
- decay_rate: float32 [32], P('tp'), may hold values from 0.0009765625 to 0.048828125
- conv_x: float32 [4, 2048], P(None, 'tp'), may hold values from -3 to 3
- conv_bc: float32 [4, 256], replicated, may hold values from -3 to 3
- skip_gain: float32 [32], P('tp'), may hold values from 0.5 to 1.5
- gate_gain: float32 [2048], P('tp'), may hold values from 0.5 to 1.5
- w_out: bfloat16 [2048, 2048], P('tp'), may hold values from -0.125 to 0.125
- attn_gain: float32 [4096], replicated, may hold values from 0.5 to 1.5
- w_qkv: bfloat16 [4096, 3, 2048], P(None, None, 'tp'), may hold values from -0.375 to 0.375
- adapter_down: bfloat16 [4096, 384], P('tp'), may hold values from -0.09375 to 0.09375
- adapter_up: bfloat16 [3, 128, 2048], P(None, None, 'tp'), may hold values from -0.5 to 0.5
- w_o: bfloat16 [2048, 2048], P('tp'), may hold values from -0.125 to 0.125
Outputs:
- hidden_out: bfloat16 [8192, 2048], P('req', 'tp')
- ssm_states: float32 [32, 32, 64, 128], P('req', 'tp')
- kv_cache: bfloat16 [8192, 2, 2048], P('req', None, 'tp')
The draws below stay inside these ranges and needn't reach their ends.
Inputs may be any that keep to these rules, and one draw needn't show every extreme that they name: `seg_ids`: segment ids never fall; each of the 16 requests holds 1 to 2048 consecutive tokens and one holds exactly 2048.
All inputs are finite; a program needn't handle non-finite values.
Results may differ from the reference program's by a relative error of at most 0.013.
Values may be sent and summed in bfloat16 or wider, within the bound.
No kernel may reach another device: no remote copies, remote signals or barrier semaphores. Data moves between devices by JAX's collectives and lax.ppermute only.
A program may use at most 128 MiB of HBM per device.

```python
import math
import jax
import jax.numpy as jnp
import numpy as np
from jax import lax

D = 2048
MINNER = 2048
HDIM = 64
STATE = 128
CONV = 4
AHEADS = 16
AHD = 128
RANK = 128
TOK_DEV = 256
REQS = 16
MHEADS = 32
AWIDTH = 4096
TOKENS = 8192
MOST = 2048


def draw_w_qkv(key, part):
    base_key = jax.random.fold_in(jax.random.fold_in(key, 7), 0)
    scale = AWIDTH ** (-0.5)
    base = jax.random.truncated_normal(base_key, -6.0, 6.0, (AWIDTH, 3, AHEADS * AHD), jnp.float32) * scale
    return jnp.clip(base, -24.0 * scale, 24.0 * scale).astype(jnp.bfloat16)


def block_scale(rng, extent, cuts, least, high):
    loudness = 1.0
    for axis_at, blocks in cuts:
        steps = jax.random.uniform(jax.random.fold_in(jax.random.fold_in(rng, 6), axis_at), (blocks,), jnp.float32, least / len(cuts), high / len(cuts))
        loudness = loudness * jnp.repeat(jnp.exp(steps), extent[axis_at] // blocks).reshape((-1,) + (1,) * (len(extent) - 1 - axis_at))
    return loudness


def split_up(count, total, most, slope):
    weights = [(1 << 20) // math.isqrt(rank ** slope) + 1 for rank in range(2, count + 1)]
    spare, given = total - most - (count - 1), [1] * (count - 1)
    while spare > 0:
        movable = [i for i in range(count - 1) if given[i] < most]
        mass, budget = sum([weights[i] for i in movable]), spare
        for i in movable:
            more = min(most - given[i], max(1, budget * weights[i] // mass), spare)
            given[i] = given[i] + more
            spare = spare - more
    return np.array([most] + given)


def uneven(key, number_of, total, most, skew):
    if number_of == 2:
        one = jax.random.randint(key, (), max(1, total - most), min(most, total - 1) + 1)
        return jnp.stack([one, total - one])
    sizes = jnp.asarray(split_up(number_of, total, most, skew), jnp.int32)
    pairs = (number_of - 1) // 2
    source_of, receiver = sizes[1:1 + 2 * pairs:2], sizes[2:2 + 2 * pairs:2]
    room = jnp.minimum(source_of - 1, most - receiver)
    moved = jax.random.randint(jax.random.fold_in(key, 1), (pairs,), 0, 1 << 20) % (room + 1)
    sizes = sizes.at[1:1 + 2 * pairs:2].set(source_of - moved).at[2:2 + 2 * pairs:2].set(receiver + moved)
    return sizes[jax.random.permutation(jax.random.fold_in(key, 2), number_of)]


def bell_draw(stream_key, shape, width, most, cuts=(), kind=jnp.bfloat16):
    values = jax.random.normal(stream_key, shape, jnp.float32) * width
    if len(cuts) > 0:
        values = block_scale(stream_key, shape, cuts, -0.22, 0.18) * values
    return jnp.clip(values, min=-most, max=most).astype(kind)


def setup_inputs(seed: int = 0) -> dict:
    seeds = jax.random.split(jax.random.key(seed), 21)
    hidden_in = bell_draw(seeds[0], (TOKENS, D), 1.0, 6.0, ((0, 32), (1, 8)))
    embeds = bell_draw(seeds[1], (TOKENS, D), 1.0, 6.0, ((0, 32), (1, 8)))
    seg_ids = jnp.searchsorted(jnp.cumsum(uneven(seeds[2], REQS, TOKENS, MOST, 2)), jnp.arange(TOKENS), side="right").astype(jnp.int32)
    mamba_gain = jnp.clip(1.0 + 0.1 * jax.random.normal(seeds[3], (D,), jnp.float32), 0.5, 1.5)
    w_z = bell_draw(seeds[4], (D, MINNER), D ** -0.5, 0.125, ((1, 8),))
    w_x = bell_draw(seeds[5], (D, MINNER), D ** -0.5, 0.125, ((1, 8),))
    w_bc = bell_draw(seeds[6], (D, 2 * STATE), D ** -0.5, 0.125, ((0, 8),))
    w_dt = bell_draw(seeds[7], (D, MHEADS), D ** -0.5, 0.125, ((1, 8),))
    dt_bias = jnp.clip(-2.0 + 2.0 * jax.random.uniform(seeds[8], (MHEADS,), jnp.float32) ** block_scale(seeds[8], (MHEADS,), ((0, 8),), -0.2, 0.2), -2.0, 0.0)
    decay_rate = jnp.clip(jnp.exp(math.log(0.048828125) - 3.912023 * jax.random.uniform(seeds[9], (MHEADS,), jnp.float32) ** block_scale(seeds[9], (MHEADS,), ((0, 8),), -0.2, 0.2)), 0.0009765625, 0.048828125)
    conv_x = bell_draw(seeds[10], (CONV, MINNER), 0.5, 3.0, ((1, 8),), jnp.float32)
    conv_bc = bell_draw(seeds[11], (CONV, 2 * STATE), 0.5, 3.0, (), jnp.float32)
    skip_gain = jnp.clip(0.5 + 1.0 * jax.random.uniform(seeds[12], (MHEADS,), jnp.float32) ** block_scale(seeds[12], (MHEADS,), ((0, 8),), -0.2, 0.2), 0.5, 1.5)
    gate_gain = jnp.clip(1.0 + 0.1 * jax.random.normal(seeds[13], (MINNER,), jnp.float32), 0.5, 1.5)
    w_out = bell_draw(seeds[14], (MINNER, D), MINNER ** -0.5, 0.125, ((0, 8),))
    attn_gain = jnp.clip(1.0 + 0.1 * jax.random.normal(seeds[15], (AWIDTH,), jnp.float32), 0.5, 1.5)
    w_qkv = draw_w_qkv(jax.random.fold_in(seeds[20], 71), 0)
    adapter_down = bell_draw(seeds[17], (AWIDTH, 3 * RANK), AWIDTH ** -0.5, 0.09375, ((0, 8),))
    adapter_up = bell_draw(seeds[18], (3, RANK, AHEADS * AHD), RANK ** -0.5, 0.5, ((2, 8),))
    w_o = bell_draw(seeds[19], (AHEADS * AHD, D), (AHEADS * AHD) ** -0.5, 0.125, ((0, 8),))
    return {"hidden_in": hidden_in, "embeds": embeds, "seg_ids": seg_ids, "mamba_gain": mamba_gain, "w_z": w_z, "w_x": w_x, "w_bc": w_bc, "w_dt": w_dt, "dt_bias": dt_bias, "decay_rate": decay_rate, "conv_x": conv_x, "conv_bc": conv_bc, "skip_gain": skip_gain, "gate_gain": gate_gain, "w_out": w_out, "attn_gain": attn_gain, "w_qkv": w_qkv, "adapter_down": adapter_down, "adapter_up": adapter_up, "w_o": w_o}


highest = lax.Precision.HIGHEST
epsilon = 1e-05

def rms_rows(values, gain):
    values = values.astype(jnp.float32)
    factor = lax.rsqrt(lax.optimization_barrier(jnp.mean(values * values, axis=-1, keepdims=True)) + epsilon)
    return values * factor * gain.astype(jnp.float32)

def positions_of(seg_all):
    total_rows = seg_all.shape[0]
    indices = jnp.arange(total_rows, dtype=jnp.int32)
    begins = jnp.concatenate([jnp.ones((1,), dtype=bool), seg_all[1:] != seg_all[:-1]])
    first_index = lax.cummax(jnp.where(begins, indices, jnp.zeros_like(indices)), axis=0)
    return indices - first_index

def rotate(values, places):
    half_dim = values.shape[-1] // 2
    freqs = jnp.exp(-jnp.log(10000.0) * jnp.arange(half_dim, dtype=jnp.float32) / half_dim)
    angles = places.astype(jnp.float32)[:, None] * freqs[None, :]
    cosine = jnp.cos(angles)[:, None, :]
    sine = jnp.sin(angles)[:, None, :]
    first_half = values[..., :half_dim]
    second_half = values[..., half_dim:]
    return jnp.concatenate([first_half * cosine - second_half * sine, second_half * cosine + first_half * sine], axis=-1)

def conv_rows(extended, seg_extended, kernel, seg_now):
    kernel_len = kernel.shape[0]
    rows_out = seg_now.shape[0]
    result = jnp.zeros((rows_out, extended.shape[1]), jnp.float32)
    for offset in range(kernel_len):
        window_rows = extended[offset:offset + rows_out]
        matches = (seg_extended[offset:offset + rows_out] == seg_now)[:, None]
        result = result + jnp.where(matches, window_rows * kernel[offset][None, :], 0.0)
    return jax.nn.silu(result)

def ssd_block(inner, write_rows, read_rows, steps_dt, log_decay, seg_block, seg_before, state_prev, skip_gain):
    length = inner.shape[0]
    cumul = jnp.cumsum(log_decay, axis=0)
    order = jnp.arange(length, dtype=jnp.int32)
    within = (seg_block[:, None] == seg_block[None, :]) & (order[:, None] >= order[None, :])
    spread = cumul.T[:, :, None] - cumul.T[:, None, :]
    decays = jnp.where(within[None], jnp.exp(jnp.minimum(spread, 0.0)), 0.0)
    intersection = jnp.dot(read_rows, write_rows.T, precision=highest)
    mixing = decays * intersection[None] * steps_dt.T[:, None, :]
    local_out = jnp.einsum('hts,shp->thp', mixing, inner, precision=highest)
    carried = jnp.where((seg_block == seg_before)[:, None], jnp.exp(cumul), 0.0)
    from_state = jnp.einsum('tn,hpn->thp', read_rows, state_prev, precision=highest)
    outputs = local_out + carried[:, :, None] * from_state + skip_gain[None, :, None] * inner
    tail_weight = jnp.where((seg_block == seg_block[-1])[:, None], jnp.exp(cumul[-1][None, :] - cumul), 0.0) * steps_dt
    keep_factor = jnp.where(seg_block[-1] == seg_before, jnp.exp(cumul[-1]), 0.0)
    state_next = keep_factor[:, None, None] * state_prev + jnp.einsum('sh,shp,sn->hpn', tail_weight, inner, write_rows, precision=highest)
    return (outputs, state_next)

def reference(hidden_in, embeds, seg_ids, mamba_gain, w_z, w_x, w_bc, w_dt, dt_bias, decay_rate, conv_x, conv_bc, skip_gain, gate_gain, w_out, attn_gain, w_qkv, adapter_down, adapter_up, w_o):
    total_rows = hidden_in.shape[0]
    normed = rms_rows(hidden_in, mamba_gain).astype(jnp.bfloat16)
    gate_z = jnp.dot(normed, w_z, preferred_element_type=jnp.float32)
    inner_x = jnp.dot(normed, w_x, preferred_element_type=jnp.float32)
    state_io = jnp.dot(normed, w_bc, preferred_element_type=jnp.float32)
    raw_dt = jnp.dot(normed, w_dt, preferred_element_type=jnp.float32)
    mixed_in = jnp.concatenate([inner_x, state_io], axis=1)
    pad_rows = CONV - 1
    extended = jnp.concatenate([jnp.zeros((pad_rows, mixed_in.shape[1]), jnp.float32), mixed_in], axis=0)
    seg_extended = jnp.concatenate([jnp.full((pad_rows,), -1, dtype=jnp.int32), seg_ids], axis=0)
    kernel = jnp.concatenate([conv_x, conv_bc], axis=1).astype(jnp.float32)
    conv_out = conv_rows(extended, seg_extended, kernel, seg_ids)
    inner_c = conv_out[:, :MINNER]
    write_rows = conv_out[:, MINNER:MINNER + STATE]
    read_rows = conv_out[:, MINNER + STATE:]
    steps_dt = jax.nn.softplus(raw_dt + dt_bias.astype(jnp.float32))
    log_decay = -steps_dt * decay_rate.astype(jnp.float32)
    blocks = total_rows // TOK_DEV
    seg_blocks = seg_ids.reshape(blocks, TOK_DEV)
    block_before = jnp.concatenate([jnp.full((1,), -1, dtype=jnp.int32), seg_blocks[:-1, -1]], axis=0)
    skip_values = skip_gain.astype(jnp.float32)

    def advance(state_prev, pieces):
        blk_inner, blk_write, blk_read, blk_dt, blk_decay, blk_seg, blk_before = pieces
        outputs, state_next = ssd_block(blk_inner, blk_write, blk_read, blk_dt, blk_decay, blk_seg, blk_before, state_prev, skip_values)
        return (state_next, (outputs, state_next))
    init_state = jnp.zeros((MHEADS, HDIM, STATE), jnp.float32)
    last_state, (block_out, ssm_states) = lax.scan(advance, init_state, (inner_c.reshape(blocks, TOK_DEV, MHEADS, HDIM), write_rows.reshape(blocks, TOK_DEV, STATE), read_rows.reshape(blocks, TOK_DEV, STATE), steps_dt.reshape(blocks, TOK_DEV, MHEADS), log_decay.reshape(blocks, TOK_DEV, MHEADS), seg_blocks, block_before))
    ssm_y = block_out.reshape(total_rows, MINNER)
    gated_rows = ssm_y * jax.nn.silu(gate_z)
    gated_norm = rms_rows(gated_rows, gate_gain).astype(jnp.bfloat16)
    mix_terms = jnp.dot(gated_norm, w_out, preferred_element_type=jnp.float32)
    hidden_mid = (hidden_in.astype(jnp.float32) + mix_terms).astype(jnp.bfloat16)
    joined = jnp.concatenate([hidden_mid, embeds], axis=1)
    attn_in = rms_rows(joined, attn_gain).astype(jnp.bfloat16)
    low_rank = jnp.dot(attn_in, adapter_down, preferred_element_type=jnp.float32).astype(jnp.bfloat16)
    cols_all = AHEADS * AHD
    projected = jnp.dot(attn_in, w_qkv.reshape(AWIDTH, 3 * cols_all), preferred_element_type=jnp.float32).reshape(total_rows, 3, cols_all)
    projected = projected + jnp.einsum('tjr,jrc->tjc', low_rank.astype(jnp.float32).reshape(total_rows, 3, RANK), adapter_up.astype(jnp.float32))
    places = positions_of(seg_ids)
    queries = rotate(projected[:, 0].reshape(total_rows, AHEADS, AHD), places).astype(jnp.bfloat16)
    key_rows = rotate(projected[:, 1].reshape(total_rows, AHEADS, AHD), places).astype(jnp.bfloat16)
    value_rows = projected[:, 2].astype(jnp.bfloat16)
    kv_cache = jnp.stack([key_rows.reshape(total_rows, cols_all), value_rows], axis=1)
    query_block = math.gcd(512, total_rows)
    key_index = jnp.arange(total_rows, dtype=jnp.int32)
    keys_f = key_rows.astype(jnp.float32)
    values_f = value_rows.reshape(total_rows, AHEADS, AHD).astype(jnp.float32)
    inv_root = 1.0 / math.sqrt(AHD)

    def attend(block_index):
        first_row = (block_index * query_block).astype(jnp.int32)
        query_blk = lax.dynamic_slice_in_dim(queries, first_row, query_block, 0).astype(jnp.float32)
        seg_query = lax.dynamic_slice_in_dim(seg_ids, first_row, query_block, 0)
        query_index = first_row + jnp.arange(query_block, dtype=jnp.int32)
        allowed = (seg_query[:, None] == seg_ids[None, :]) & (key_index[None, :] <= query_index[:, None])
        scores = jnp.einsum('qhe,khe->hqk', query_blk, keys_f) * inv_root
        masked = jnp.where(allowed[None], scores, -1e+30)
        row_top = lax.optimization_barrier(jnp.max(masked, axis=-1, keepdims=True))
        weights = jnp.where(allowed[None], jnp.exp(scores - row_top), 0.0)
        denom_sum = lax.optimization_barrier(jnp.sum(weights, axis=-1))
        probs = weights.astype(jnp.bfloat16).astype(jnp.float32)
        summed = jnp.einsum('hqk,khe->qhe', probs, values_f)
        return (summed / denom_sum.T[:, :, None]).astype(jnp.bfloat16)
    attended = lax.map(attend, jnp.arange(total_rows // query_block, dtype=jnp.int32)).reshape(total_rows, cols_all)
    attn_terms = jnp.dot(attended, w_o, preferred_element_type=jnp.float32)
    hidden_out = (hidden_mid.astype(jnp.float32) + attn_terms).astype(jnp.bfloat16)
    return (hidden_out, ssm_states, kv_cache)
```

```python
import math

import jax
import jax.numpy as jnp
from jax import lax
from jax.sharding import PartitionSpec as P

AHD = 128


highest = lax.Precision.HIGHEST
epsilon = 1e-05


def from_behind(block, axis, distance):
    devices = range(lax.axis_size(axis))
    route = [(i - distance, i) for i in devices if i - distance in devices]
    return lax.ppermute(block, axis, route)


def carried_in_2(value, axis, join, neutral):
    count, mine = (lax.axis_size(axis), lax.axis_index(axis))
    pieces = jax.tree.map(lambda part: lax.all_gather(part, axis), value)
    so_far = jax.tree.map(
        lambda part, zero: jnp.full_like(part, 0) + jnp.asarray(zero, part.dtype), value, neutral
    )

    def lap(position, so_far):
        longer = join(so_far, jax.tree.map(lambda part: part[position], pieces))
        return jax.tree.map(lambda new, old: jnp.where(position < mine, new, old), longer, so_far)

    return lax.fori_loop(0, count - 1, lap, so_far)


MOST = 2048


def shifted(block, axis, distance):
    count = lax.axis_size(axis)
    return lax.ppermute(block, axis, [(i, (i + distance) % count) for i in range(count)])


def tp_layout():
    count = lax.axis_size("tp")
    inner = 2 if count % 2 == 0 else 1
    return count, inner, count // inner


def tp_gather(block, axis):
    count, inner, outer = tp_layout()
    rank = lax.axis_index("tp")
    outer_rank, inner_rank = rank // inner, rank % inner
    width = block.shape[axis]
    sources = [block]
    if inner == 2:
        sources.append(lax.ppermute(block, "tp", [(i, i ^ 1) for i in range(count)]))
    full_shape = list(block.shape)
    full_shape[axis] = width * count
    full = jnp.zeros(full_shape, block.dtype)
    for which, source in enumerate(sources):
        source_inner = (inner_rank + which) % inner
        for step in range(outer):
            piece = source if step == 0 else shifted(source, "tp", inner * step)
            place = ((outer_rank - step) % outer) * inner + source_inner
            full = lax.dynamic_update_slice_in_dim(full, piece, place * width, axis)
    return full


def tp_scatter(values, send_dtype):
    count, inner, outer = tp_layout()
    rank = lax.axis_index("tp")
    outer_rank, inner_rank = rank // inner, rank % inner
    width = values.shape[1] // count
    span = inner * width
    total = lax.dynamic_slice_in_dim(values, outer_rank * span, span, 1).astype(jnp.float32)
    for step in range(1, outer):
        piece = lax.dynamic_slice_in_dim(values, ((outer_rank + step) % outer) * span, span, 1)
        total = total + shifted(piece.astype(send_dtype), "tp", inner * step).astype(jnp.float32)
    mine = lax.dynamic_slice_in_dim(total, inner_rank * width, width, 1)
    if inner == 2:
        theirs = lax.dynamic_slice_in_dim(total, (1 - inner_rank) * width, width, 1)
        swapped = lax.ppermute(theirs.astype(send_dtype), "tp", [(i, i ^ 1) for i in range(count)])
        mine = mine + swapped.astype(jnp.float32)
    return mine


def carried_in_scan(through, state, reach):
    rank = lax.axis_index("req")
    valid = rank >= 1
    carry_t = jnp.where(valid, from_behind(through, "req", 1), 1.0)
    carry_s = jnp.where(valid, from_behind(state, "req", 1), 0.0)
    distance = 1
    while distance < reach:
        prev_t, prev_s = from_behind((carry_t, carry_s), "req", distance)
        joined_t, joined_s = combine_states((prev_t, prev_s), (carry_t, carry_s))
        keep = rank >= distance
        carry_t = jnp.where(keep, joined_t, carry_t)
        carry_s = jnp.where(keep, joined_s, carry_s)
        distance *= 2
    return carry_s


def rms_rows(values, gain):
    values = values.astype(jnp.float32)
    factor = lax.rsqrt(jnp.mean(values * values, axis=-1, keepdims=True) + epsilon)
    return values * factor * gain


def positions_of(seg_all):
    total_rows = seg_all.shape[0]
    indices = jnp.arange(total_rows, dtype=jnp.int32)
    begins = jnp.concatenate([jnp.ones((1,), dtype=bool), seg_all[1:] != seg_all[:-1]])
    first_index = lax.cummax(jnp.where(begins, indices, jnp.zeros_like(indices)), axis=0)
    return indices - first_index


def rotate(values, places):
    half_dim = values.shape[-1] // 2
    freqs = jnp.exp(-jnp.log(10000.0) * jnp.arange(half_dim, dtype=jnp.float32) / half_dim)
    angles = places.astype(jnp.float32)[:, None] * freqs[None, :]
    cosine = jnp.cos(angles)[:, None, :]
    sine = jnp.sin(angles)[:, None, :]
    first_half = values[..., :half_dim]
    second_half = values[..., half_dim:]
    return jnp.concatenate(
        [first_half * cosine - second_half * sine, second_half * cosine + first_half * sine],
        axis=-1,
    )


def conv_rows(extended, seg_extended, kernel, seg_now):
    kernel_len = kernel.shape[0]
    rows_out = seg_now.shape[0]
    result = jnp.zeros((rows_out, extended.shape[1]), jnp.float32)
    for offset in range(kernel_len):
        window_rows = extended[offset : offset + rows_out]
        matches = (seg_extended[offset : offset + rows_out] == seg_now)[:, None]
        result = result + jnp.where(matches, window_rows * kernel[offset][None, :], 0.0)
    return jax.nn.silu(result)


def ssd_block(
    inner, write_rows, read_rows, steps_dt, log_decay, seg_block, seg_before, state_prev, skip_gain
):
    length = inner.shape[0]
    cumul = jnp.cumsum(log_decay, axis=0)
    order = jnp.arange(length, dtype=jnp.int32)
    within = (seg_block[:, None] == seg_block[None, :]) & (order[:, None] >= order[None, :])
    spread = cumul.T[:, :, None] - cumul.T[:, None, :]
    decays = jnp.where(within[None], jnp.exp(jnp.minimum(spread, 0.0)), 0.0)
    intersection = jnp.dot(read_rows, write_rows.T, precision=highest)
    mixing = decays * intersection[None] * steps_dt.T[:, None, :]
    local_out = jnp.einsum("hts,shp->thp", mixing, inner, precision=highest)
    carried = jnp.where((seg_block == seg_before)[:, None], jnp.exp(cumul), 0.0)
    from_state = jnp.einsum("tn,hpn->thp", read_rows, state_prev, precision=highest)
    outputs = local_out + carried[:, :, None] * from_state + skip_gain[None, :, None] * inner
    tail_weight = (
        jnp.where((seg_block == seg_block[-1])[:, None], jnp.exp(cumul[-1][None, :] - cumul), 0.0)
        * steps_dt
    )
    keep_factor = jnp.where(seg_block[-1] == seg_before, jnp.exp(cumul[-1]), 0.0)
    state_next = keep_factor[:, None, None] * state_prev + jnp.einsum(
        "sh,shp,sn->hpn", tail_weight, inner, write_rows, precision=highest
    )
    return (outputs, state_next)


def accumulate_rows(left_rows, weight_rows):
    return jnp.dot(left_rows, weight_rows, preferred_element_type=jnp.float32)


def combine_states(earlier, later):
    return (earlier[0] * later[0], later[0][:, None, None] * earlier[1] + later[1])


def on_device(
    hidden_in,
    embeds,
    seg_ids,
    mamba_gain,
    w_z,
    w_x,
    w_bc,
    w_dt,
    dt_bias,
    decay_rate,
    conv_x,
    conv_bc,
    skip_gain,
    gate_gain,
    w_out,
    attn_gain,
    w_qkv,
    adapter_down,
    adapter_up,
    w_o,
):
    rows_here = hidden_in.shape[0]
    tensor_size = lax.axis_size("tp")
    req_rank = lax.axis_index("req")
    first_row = req_rank * rows_here
    full_hidden = tp_gather(hidden_in, 1)
    full_embeds = tp_gather(embeds, 1)
    normed = rms_rows(full_hidden, mamba_gain).astype(jnp.bfloat16)
    gate_z = jnp.dot(normed, w_z, preferred_element_type=jnp.float32)
    inner_x = jnp.dot(normed, w_x, preferred_element_type=jnp.float32)
    raw_dt = jnp.dot(normed, w_dt, preferred_element_type=jnp.float32)
    state_io = accumulate_rows(normed, tp_gather(w_bc, 0))
    mixed_in = jnp.concatenate([inner_x, state_io], axis=1)
    kernel_len = conv_x.shape[0]
    tail_rows = mixed_in[rows_here - (kernel_len - 1) :]
    prior_rows = from_behind(tail_rows, "req", 1)
    extended = jnp.concatenate([prior_rows, mixed_in], axis=0)
    seg_padded = jnp.concatenate(
        [jnp.full((kernel_len - 1,), -1, dtype=jnp.int32), seg_ids], axis=0
    )
    seg_extended = lax.dynamic_slice_in_dim(seg_padded, first_row, rows_here + kernel_len - 1, 0)
    seg_now = lax.dynamic_slice_in_dim(seg_ids, first_row, rows_here, 0)
    kernel = jnp.concatenate([conv_x, conv_bc], axis=1)
    conv_out = conv_rows(extended, seg_extended, kernel, seg_now)
    inner_here = w_z.shape[1]
    heads_here = w_dt.shape[1]
    head_dim = inner_here // heads_here
    state_dim = state_io.shape[1] // 2
    inner_c = conv_out[:, :inner_here].reshape(rows_here, heads_here, head_dim)
    write_rows = conv_out[:, inner_here : inner_here + state_dim]
    read_rows = conv_out[:, inner_here + state_dim :]
    steps_dt = jax.nn.softplus(raw_dt + dt_bias)
    log_decay = -steps_dt * decay_rate
    seg_before = jnp.where(req_rank > 0, seg_ids[jnp.maximum(first_row - 1, 0)], -1)
    seg_prior = jnp.concatenate([seg_before[None], seg_now[:-1]], axis=0)
    block_rows = math.gcd(rows_here, 256)
    count_blocks = rows_here // block_rows
    block_before = seg_prior.reshape(count_blocks, block_rows)[:, 0]

    def ssd_step(state_prev, pieces):
        blk_inner, blk_write, blk_read, blk_dt, blk_decay, blk_seg, blk_before = pieces
        outputs, state_next = ssd_block(
            blk_inner,
            blk_write,
            blk_read,
            blk_dt,
            blk_decay,
            blk_seg,
            blk_before,
            state_prev,
            skip_gain,
        )
        return (state_next, outputs)

    zero_state = jnp.zeros((heads_here, head_dim, state_dim), jnp.float32)
    local_state, local_out = lax.scan(
        ssd_step,
        zero_state,
        (
            inner_c.reshape(count_blocks, block_rows, heads_here, head_dim),
            write_rows.reshape(count_blocks, block_rows, state_dim),
            read_rows.reshape(count_blocks, block_rows, state_dim),
            steps_dt.reshape(count_blocks, block_rows, heads_here),
            log_decay.reshape(count_blocks, block_rows, heads_here),
            seg_now.reshape(count_blocks, block_rows),
            block_before,
        ),
    )
    local_out = local_out.reshape(rows_here, heads_here, head_dim)
    cumul_all = jnp.cumsum(log_decay, axis=0)
    through = jnp.where(seg_now[-1] == seg_before, jnp.exp(cumul_all[-1]), 0.0)
    carried_in = carried_in_scan(through, local_state, -(-MOST // rows_here))
    carried = jnp.where((seg_now == seg_before)[:, None], jnp.exp(cumul_all), 0.0)
    from_state = jnp.einsum("tn,hpn->thp", read_rows, carried_in, precision=highest)
    ssm_y = local_out + carried[:, :, None] * from_state
    final_state = local_state + through[:, None, None] * carried_in
    gated_rows = ssm_y.reshape(rows_here, inner_here) * jax.nn.silu(gate_z)
    square_parts = tp_gather(jnp.sum(gated_rows * gated_rows, axis=1, keepdims=True), 1)
    square_sum = jnp.sum(square_parts, axis=1)
    factor = lax.rsqrt(square_sum / (inner_here * tensor_size) + epsilon)
    gained = (gated_rows * gate_gain).astype(jnp.bfloat16)
    mix_terms = jnp.dot(gained, w_out, preferred_element_type=jnp.float32)
    mix_share = tp_scatter(mix_terms, jnp.float32) * factor[:, None]
    mid_here = (hidden_in.astype(jnp.float32) + mix_share).astype(jnp.bfloat16)
    mid_full = tp_gather(mid_here, 1)
    joined = jnp.concatenate([mid_full, full_embeds], axis=1)
    attn_in = rms_rows(joined, attn_gain).astype(jnp.bfloat16)
    low_sum = accumulate_rows(attn_in, tp_gather(adapter_down, 0))
    low_rank = low_sum.astype(jnp.bfloat16)
    rank_cols = adapter_up.shape[1]
    cols_here = w_qkv.shape[2]
    heads_attn = cols_here // AHD
    projected = jnp.dot(
        attn_in, w_qkv.reshape(w_qkv.shape[0], 3 * cols_here), preferred_element_type=jnp.float32
    ).reshape(rows_here, 3, cols_here)
    projected = projected + jnp.einsum(
        "tjr,jrc->tjc",
        low_rank.reshape(rows_here, 3, rank_cols),
        adapter_up,
        preferred_element_type=jnp.float32,
    )
    places = lax.dynamic_slice_in_dim(positions_of(seg_ids), first_row, rows_here, 0)
    queries = rotate(projected[:, 0].reshape(rows_here, heads_attn, AHD), places).astype(
        jnp.bfloat16
    )
    key_rows = rotate(projected[:, 1].reshape(rows_here, heads_attn, AHD), places).astype(
        jnp.bfloat16
    )
    value_rows = projected[:, 2].astype(jnp.bfloat16)
    kv_pair = jnp.stack([key_rows.reshape(rows_here, cols_here), value_rows], axis=1)
    query_index = first_row + jnp.arange(rows_here, dtype=jnp.int32)
    inv_root = 1.0 / math.sqrt(AHD)

    def absorb(running, block_kv, first_key):
        row_top, denom_sum, weighted = running
        key_count = block_kv.shape[0]
        key_index = first_key + jnp.arange(key_count, dtype=jnp.int32)
        key_seg = lax.dynamic_slice_in_dim(seg_ids, jnp.maximum(first_key, 0), key_count, 0)
        allowed = (
            (key_seg[None, :] == seg_now[:, None])
            & (key_index[None, :] <= query_index[:, None])
            & (key_index[None, :] >= 0)
        )
        block_keys = block_kv[:, 0].reshape(key_count, heads_attn, AHD)
        block_vals = block_kv[:, 1].reshape(key_count, heads_attn, AHD)
        scores = (
            jnp.einsum("qhe,khe->hqk", queries, block_keys, preferred_element_type=jnp.float32)
            * inv_root
        )
        masked = jnp.where(allowed[None], scores, -1e30)
        new_top = jnp.maximum(row_top, jnp.max(masked, axis=-1))
        weights = jnp.where(allowed[None], jnp.exp(scores - new_top[:, :, None]), 0.0)
        shrink = jnp.exp(row_top - new_top)
        denom_sum = denom_sum * shrink + jnp.sum(weights, axis=-1)
        weighted = weighted * shrink[:, :, None] + jnp.einsum(
            "hqk,khe->hqe",
            weights.astype(jnp.bfloat16),
            block_vals,
            preferred_element_type=jnp.float32,
        )
        return (new_top, denom_sum, weighted)

    start_state = (
        jnp.full((heads_attn, rows_here), -1e30, jnp.float32),
        jnp.zeros((heads_attn, rows_here), jnp.float32),
        jnp.zeros((heads_attn, rows_here, AHD), jnp.float32),
    )
    reach_hops = min(lax.axis_size("req") - 1, -(-(MOST - 1) // rows_here))
    running = absorb(start_state, kv_pair, first_row)
    for hop_count in range(1, reach_hops + 1):
        moving = from_behind(kv_pair, "req", hop_count)
        running = absorb(running, moving, first_row - hop_count * rows_here)
    row_top, denom_sum, weighted = running
    attended = (weighted / denom_sum[:, :, None]).astype(jnp.bfloat16)
    attended = attended.transpose(1, 0, 2).reshape(rows_here, cols_here)
    attn_terms = jnp.dot(attended, w_o, preferred_element_type=jnp.float32)
    attn_share = tp_scatter(attn_terms, jnp.bfloat16)
    hidden_out = (mid_here.astype(jnp.float32) + attn_share).astype(jnp.bfloat16)
    return (hidden_out, final_state[None], kv_pair)


def solution(mesh):
    in_specs = (
        P("req", "tp"),
        P("req", "tp"),
        P(),
        P(),
        P(None, "tp"),
        P(None, "tp"),
        P("tp", None),
        P(None, "tp"),
        P("tp"),
        P("tp"),
        P(None, "tp"),
        P(),
        P("tp"),
        P("tp"),
        P("tp", None),
        P(),
        P(None, None, "tp"),
        P("tp", None),
        P(None, None, "tp"),
        P("tp", None),
    )
    out_specs = (P("req", "tp"), P("req", "tp", None, None), P("req", None, "tp"))
    return jax.shard_map(
        on_device, mesh=mesh, in_specs=in_specs, out_specs=out_specs, check_vma=False
    )
```

```python
import math

import jax
import jax.numpy as jnp
from jax import lax
from jax.sharding import PartitionSpec as P

AHD = 128


highest = lax.Precision.HIGHEST
epsilon = 1e-05


def from_behind(block, axis, distance):
    devices = range(lax.axis_size(axis))
    route = [(i - distance, i) for i in devices if i - distance in devices]
    return lax.ppermute(block, axis, route)


def carried_in_2(value, axis, join, neutral):
    count, mine = (lax.axis_size(axis), lax.axis_index(axis))
    pieces = jax.tree.map(lambda part: lax.all_gather(part, axis), value)
    so_far = jax.tree.map(
        lambda part, zero: jnp.full_like(part, 0) + jnp.asarray(zero, part.dtype), value, neutral
    )

    def lap(position, so_far):
        longer = join(so_far, jax.tree.map(lambda part: part[position], pieces))
        return jax.tree.map(lambda new, old: jnp.where(position < mine, new, old), longer, so_far)

    return lax.fori_loop(0, count - 1, lap, so_far)


MOST = 2048


def shifted(block, axis, distance):
    count = lax.axis_size(axis)
    return lax.ppermute(block, axis, [(i, (i + distance) % count) for i in range(count)])


def tp_layout():
    count = lax.axis_size("tp")
    inner = 2 if count % 2 == 0 else 1
    return count, inner, count // inner


def tp_blocks(block):
    count, inner, outer = tp_layout()
    rank = lax.axis_index("tp")
    outer_rank, inner_rank = rank // inner, rank % inner
    if inner == 2:
        partner = lax.ppermute(block, "tp", [(i, i ^ 1) for i in range(count)])
        low = jnp.where(inner_rank == 0, block, partner)
        high = jnp.where(inner_rank == 0, partner, block)
        pair = jnp.stack([low, high])
    else:
        pair = block[None]
    slots = jnp.stack([pair] + [shifted(pair, "tp", inner * step) for step in range(1, outer)])
    ordered = jnp.roll(slots[::-1], outer_rank + 1, axis=0)
    return ordered.reshape((count,) + block.shape)


def tp_gather_many(arrays):
    flat = jnp.concatenate([part.reshape(-1) for part in arrays])
    blocks = tp_blocks(flat)
    count = blocks.shape[0]
    pieces, offset = ([], 0)
    for part in arrays:
        pieces.append(blocks[:, offset : offset + part.size].reshape((count,) + part.shape))
        offset += part.size
    return pieces


def rms_blocks(blocks, gain):
    values = blocks.astype(jnp.float32)
    factor = lax.rsqrt(jnp.mean(values * values, axis=(0, 2)) + epsilon)
    return values * factor[None, :, None] * gain.reshape(blocks.shape[0], 1, blocks.shape[2])


def blocked_dot(blocks, weight):
    weight = weight.reshape(blocks.shape[0], blocks.shape[2], -1)
    return jnp.einsum("ktf,kfo->to", blocks, weight, preferred_element_type=jnp.float32)


def tp_scatter(values, send_dtype):
    count, inner, outer = tp_layout()
    rank = lax.axis_index("tp")
    outer_rank, inner_rank = rank // inner, rank % inner
    width = values.shape[1] // count
    span = inner * width
    total = lax.dynamic_slice_in_dim(values, outer_rank * span, span, 1).astype(jnp.float32)
    for step in range(1, outer):
        piece = lax.dynamic_slice_in_dim(values, ((outer_rank + step) % outer) * span, span, 1)
        total = total + shifted(piece.astype(send_dtype), "tp", inner * step).astype(jnp.float32)
    mine = lax.dynamic_slice_in_dim(total, inner_rank * width, width, 1)
    if inner == 2:
        theirs = lax.dynamic_slice_in_dim(total, (1 - inner_rank) * width, width, 1)
        swapped = lax.ppermute(theirs.astype(send_dtype), "tp", [(i, i ^ 1) for i in range(count)])
        mine = mine + swapped.astype(jnp.float32)
    return mine


def carried_in_scan(through, state, reach):
    heads = through.shape[0]

    def pack(decay, value):
        return jnp.concatenate([value.reshape(-1), decay])

    def unpack(packed):
        return (packed[-heads:], packed[:-heads].reshape(state.shape))

    rank = lax.axis_index("req")
    neutral = pack(jnp.ones_like(through), jnp.zeros_like(state))
    carry = jnp.where(rank >= 1, from_behind(pack(through, state), "req", 1), neutral)
    distance = 1
    while distance < reach:
        prev = from_behind(carry, "req", distance)
        joined = pack(*combine_states(unpack(prev), unpack(carry)))
        carry = jnp.where(rank >= distance, joined, carry)
        distance *= 2
    return unpack(carry)[1]


def rms_rows(values, gain):
    values = values.astype(jnp.float32)
    factor = lax.rsqrt(jnp.mean(values * values, axis=-1, keepdims=True) + epsilon)
    return values * factor * gain


def positions_of(seg_all):
    total_rows = seg_all.shape[0]
    indices = jnp.arange(total_rows, dtype=jnp.int32)
    begins = jnp.concatenate([jnp.ones((1,), dtype=bool), seg_all[1:] != seg_all[:-1]])
    first_index = lax.cummax(jnp.where(begins, indices, jnp.zeros_like(indices)), axis=0)
    return indices - first_index


def rotate(values, places):
    half_dim = values.shape[-1] // 2
    freqs = jnp.exp(-jnp.log(10000.0) * jnp.arange(half_dim, dtype=jnp.float32) / half_dim)
    angles = places.astype(jnp.float32)[:, None] * freqs[None, :]
    cosine = jnp.cos(angles)[:, None, :]
    sine = jnp.sin(angles)[:, None, :]
    first_half = values[..., :half_dim]
    second_half = values[..., half_dim:]
    return jnp.concatenate(
        [first_half * cosine - second_half * sine, second_half * cosine + first_half * sine],
        axis=-1,
    )


def conv_rows(extended, seg_extended, kernel, seg_now):
    kernel_len = kernel.shape[0]
    rows_out = seg_now.shape[0]
    result = jnp.zeros((rows_out, extended.shape[1]), jnp.float32)
    for offset in range(kernel_len):
        window_rows = extended[offset : offset + rows_out]
        matches = (seg_extended[offset : offset + rows_out] == seg_now)[:, None]
        result = result + jnp.where(matches, window_rows * kernel[offset][None, :], 0.0)
    return jax.nn.silu(result)


def ssd_block(
    inner, write_rows, read_rows, steps_dt, log_decay, seg_block, seg_before, state_prev, skip_gain
):
    length = inner.shape[0]
    cumul = jnp.cumsum(log_decay, axis=0)
    order = jnp.arange(length, dtype=jnp.int32)
    within = (seg_block[:, None] == seg_block[None, :]) & (order[:, None] >= order[None, :])
    spread = cumul.T[:, :, None] - cumul.T[:, None, :]
    decays = jnp.where(within[None], jnp.exp(jnp.minimum(spread, 0.0)), 0.0)
    intersection = jnp.dot(read_rows, write_rows.T, precision=highest)
    mixing = decays * intersection[None] * steps_dt.T[:, None, :]
    local_out = jnp.einsum("hts,shp->thp", mixing, inner, precision=highest)
    carried = jnp.where((seg_block == seg_before)[:, None], jnp.exp(cumul), 0.0)
    from_state = jnp.einsum("tn,hpn->thp", read_rows, state_prev, precision=highest)
    outputs = local_out + carried[:, :, None] * from_state + skip_gain[None, :, None] * inner
    tail_weight = (
        jnp.where((seg_block == seg_block[-1])[:, None], jnp.exp(cumul[-1][None, :] - cumul), 0.0)
        * steps_dt
    )
    keep_factor = jnp.where(seg_block[-1] == seg_before, jnp.exp(cumul[-1]), 0.0)
    state_next = keep_factor[:, None, None] * state_prev + jnp.einsum(
        "sh,shp,sn->hpn", tail_weight, inner, write_rows, precision=highest
    )
    return (outputs, state_next)


def accumulate_rows(left_rows, weight_rows):
    return jnp.dot(left_rows, weight_rows, preferred_element_type=jnp.float32)


def combine_states(earlier, later):
    return (earlier[0] * later[0], later[0][:, None, None] * earlier[1] + later[1])


def on_device(
    hidden_in,
    embeds,
    seg_ids,
    mamba_gain,
    w_z,
    w_x,
    w_bc,
    w_dt,
    dt_bias,
    decay_rate,
    conv_x,
    conv_bc,
    skip_gain,
    gate_gain,
    w_out,
    attn_gain,
    w_qkv,
    adapter_down,
    adapter_up,
    w_o,
):
    rows_here = hidden_in.shape[0]
    tensor_size = lax.axis_size("tp")
    req_rank = lax.axis_index("req")
    first_row = req_rank * rows_here
    hidden_blocks, w_bc_blocks = tp_gather_many([hidden_in, w_bc])
    embed_blocks, down_blocks = tp_gather_many([embeds, adapter_down])
    normed = rms_blocks(hidden_blocks, mamba_gain).astype(jnp.bfloat16)
    gate_z = blocked_dot(normed, w_z)
    inner_x = blocked_dot(normed, w_x)
    raw_dt = blocked_dot(normed, w_dt)
    state_io = blocked_dot(normed, w_bc_blocks.reshape(-1, w_bc.shape[1]))
    mixed_in = jnp.concatenate([inner_x, state_io], axis=1)
    kernel_len = conv_x.shape[0]
    tail_rows = mixed_in[rows_here - (kernel_len - 1) :]
    prior_rows = from_behind(tail_rows, "req", 1)
    extended = jnp.concatenate([prior_rows, mixed_in], axis=0)
    seg_padded = jnp.concatenate(
        [jnp.full((kernel_len - 1,), -1, dtype=jnp.int32), seg_ids], axis=0
    )
    seg_extended = lax.dynamic_slice_in_dim(seg_padded, first_row, rows_here + kernel_len - 1, 0)
    seg_now = lax.dynamic_slice_in_dim(seg_ids, first_row, rows_here, 0)
    kernel = jnp.concatenate([conv_x, conv_bc], axis=1)
    conv_out = conv_rows(extended, seg_extended, kernel, seg_now)
    inner_here = w_z.shape[1]
    heads_here = w_dt.shape[1]
    head_dim = inner_here // heads_here
    state_dim = state_io.shape[1] // 2
    inner_c = conv_out[:, :inner_here].reshape(rows_here, heads_here, head_dim)
    write_rows = conv_out[:, inner_here : inner_here + state_dim]
    read_rows = conv_out[:, inner_here + state_dim :]
    steps_dt = jax.nn.softplus(raw_dt + dt_bias)
    log_decay = -steps_dt * decay_rate
    seg_before = jnp.where(req_rank > 0, seg_ids[jnp.maximum(first_row - 1, 0)], -1)
    seg_prior = jnp.concatenate([seg_before[None], seg_now[:-1]], axis=0)
    block_rows = math.gcd(rows_here, 256)
    count_blocks = rows_here // block_rows
    block_before = seg_prior.reshape(count_blocks, block_rows)[:, 0]

    def ssd_step(state_prev, pieces):
        blk_inner, blk_write, blk_read, blk_dt, blk_decay, blk_seg, blk_before = pieces
        outputs, state_next = ssd_block(
            blk_inner,
            blk_write,
            blk_read,
            blk_dt,
            blk_decay,
            blk_seg,
            blk_before,
            state_prev,
            skip_gain,
        )
        return (state_next, outputs)

    zero_state = jnp.zeros((heads_here, head_dim, state_dim), jnp.float32)
    local_state, local_out = lax.scan(
        ssd_step,
        zero_state,
        (
            inner_c.reshape(count_blocks, block_rows, heads_here, head_dim),
            write_rows.reshape(count_blocks, block_rows, state_dim),
            read_rows.reshape(count_blocks, block_rows, state_dim),
            steps_dt.reshape(count_blocks, block_rows, heads_here),
            log_decay.reshape(count_blocks, block_rows, heads_here),
            seg_now.reshape(count_blocks, block_rows),
            block_before,
        ),
    )
    local_out = local_out.reshape(rows_here, heads_here, head_dim)
    cumul_all = jnp.cumsum(log_decay, axis=0)
    through = jnp.where(seg_now[-1] == seg_before, jnp.exp(cumul_all[-1]), 0.0)
    carried_in = carried_in_scan(through, local_state, -(-MOST // rows_here))
    carried = jnp.where((seg_now == seg_before)[:, None], jnp.exp(cumul_all), 0.0)
    from_state = jnp.einsum("tn,hpn->thp", read_rows, carried_in, precision=highest)
    ssm_y = local_out + carried[:, :, None] * from_state
    final_state = local_state + through[:, None, None] * carried_in
    gated_rows = ssm_y.reshape(rows_here, inner_here) * jax.nn.silu(gate_z)
    square_part = jnp.sum(gated_rows * gated_rows, axis=1)
    gained = (gated_rows * gate_gain).astype(jnp.bfloat16)
    mix_terms = jnp.dot(gained, w_out, preferred_element_type=jnp.float32)
    with_squares = jnp.concatenate([mix_terms, jnp.tile(square_part[None], (1, tensor_size))], axis=0)
    reduced = tp_scatter(with_squares, jnp.float32)
    factor = lax.rsqrt(reduced[rows_here] / (inner_here * tensor_size) + epsilon)
    mix_share = reduced[:rows_here] * factor[:, None]
    mid_here = (hidden_in.astype(jnp.float32) + mix_share).astype(jnp.bfloat16)
    joined = jnp.concatenate([tp_blocks(mid_here), embed_blocks], axis=0)
    attn_in = rms_blocks(joined, attn_gain).astype(jnp.bfloat16)
    low_sum = blocked_dot(attn_in, down_blocks.reshape(-1, adapter_down.shape[1]))
    low_rank = low_sum.astype(jnp.bfloat16)
    rank_cols = adapter_up.shape[1]
    cols_here = w_qkv.shape[2]
    heads_attn = cols_here // AHD
    projected = blocked_dot(attn_in, w_qkv).reshape(rows_here, 3, cols_here)
    projected = projected + jnp.einsum(
        "tjr,jrc->tjc",
        low_rank.reshape(rows_here, 3, rank_cols),
        adapter_up,
        preferred_element_type=jnp.float32,
    )
    places = lax.dynamic_slice_in_dim(positions_of(seg_ids), first_row, rows_here, 0)
    queries = rotate(projected[:, 0].reshape(rows_here, heads_attn, AHD), places).astype(
        jnp.bfloat16
    )
    key_rows = rotate(projected[:, 1].reshape(rows_here, heads_attn, AHD), places).astype(
        jnp.bfloat16
    )
    value_rows = projected[:, 2].astype(jnp.bfloat16)
    kv_pair = jnp.stack([key_rows.reshape(rows_here, cols_here), value_rows], axis=1)
    query_index = first_row + jnp.arange(rows_here, dtype=jnp.int32)
    inv_root = 1.0 / math.sqrt(AHD)

    def absorb(running, block_kv, first_key):
        row_top, denom_sum, weighted = running
        key_count = block_kv.shape[0]
        key_index = first_key + jnp.arange(key_count, dtype=jnp.int32)
        key_seg = lax.dynamic_slice_in_dim(seg_ids, jnp.maximum(first_key, 0), key_count, 0)
        allowed = (
            (key_seg[None, :] == seg_now[:, None])
            & (key_index[None, :] <= query_index[:, None])
            & (key_index[None, :] >= 0)
        )
        block_keys = block_kv[:, 0].reshape(key_count, heads_attn, AHD)
        block_vals = block_kv[:, 1].reshape(key_count, heads_attn, AHD)
        scores = (
            jnp.einsum("qhe,khe->hqk", queries, block_keys, preferred_element_type=jnp.float32)
            * inv_root
        )
        masked = jnp.where(allowed[None], scores, -1e30)
        new_top = jnp.maximum(row_top, jnp.max(masked, axis=-1))
        weights = jnp.where(allowed[None], jnp.exp(scores - new_top[:, :, None]), 0.0)
        shrink = jnp.exp(row_top - new_top)
        denom_sum = denom_sum * shrink + jnp.sum(weights, axis=-1)
        weighted = weighted * shrink[:, :, None] + jnp.einsum(
            "hqk,khe->hqe",
            weights.astype(jnp.bfloat16),
            block_vals,
            preferred_element_type=jnp.float32,
        )
        return (new_top, denom_sum, weighted)

    start_state = (
        jnp.full((heads_attn, rows_here), -1e30, jnp.float32),
        jnp.zeros((heads_attn, rows_here), jnp.float32),
        jnp.zeros((heads_attn, rows_here, AHD), jnp.float32),
    )
    reach_hops = min(lax.axis_size("req") - 1, -(-(MOST - 1) // rows_here))
    running = absorb(start_state, kv_pair, first_row)
    for hop_count in range(1, reach_hops + 1):
        moving = from_behind(kv_pair, "req", hop_count)
        running = absorb(running, moving, first_row - hop_count * rows_here)
    row_top, denom_sum, weighted = running
    attended = (weighted / denom_sum[:, :, None]).astype(jnp.bfloat16)
    attended = attended.transpose(1, 0, 2).reshape(rows_here, cols_here)
    attn_terms = jnp.dot(attended, w_o, preferred_element_type=jnp.float32)
    attn_share = tp_scatter(attn_terms, jnp.bfloat16)
    hidden_out = (mid_here.astype(jnp.float32) + attn_share).astype(jnp.bfloat16)
    return (hidden_out, final_state[None], kv_pair)


def solution(mesh):
    in_specs = (
        P("req", "tp"),
        P("req", "tp"),
        P(),
        P(),
        P(None, "tp"),
        P(None, "tp"),
        P("tp", None),
        P(None, "tp"),
        P("tp"),
        P("tp"),
        P(None, "tp"),
        P(),
        P("tp"),
        P("tp"),
        P("tp", None),
        P(),
        P(None, None, "tp"),
        P("tp", None),
        P(None, None, "tp"),
        P("tp", None),
    )
    out_specs = (P("req", "tp"), P("req", "tp", None, None), P("req", None, "tp"))
    return jax.shard_map(
        on_device, mesh=mesh, in_specs=in_specs, out_specs=out_specs, check_vma=False
    )
```

```python
import math

import jax
import jax.numpy as jnp
from jax import lax
from jax.sharding import PartitionSpec as P

AHD = 128


highest = lax.Precision.HIGHEST
epsilon = 1e-05


def from_behind(block, axis, distance):
    devices = range(lax.axis_size(axis))
    route = [(i - distance, i) for i in devices if i - distance in devices]
    return lax.ppermute(block, axis, route)


def carried_in_2(value, axis, join, neutral):
    count, mine = (lax.axis_size(axis), lax.axis_index(axis))
    pieces = jax.tree.map(lambda part: lax.all_gather(part, axis), value)
    so_far = jax.tree.map(
        lambda part, zero: jnp.full_like(part, 0) + jnp.asarray(zero, part.dtype), value, neutral
    )

    def lap(position, so_far):
        longer = join(so_far, jax.tree.map(lambda part: part[position], pieces))
        return jax.tree.map(lambda new, old: jnp.where(position < mine, new, old), longer, so_far)

    return lax.fori_loop(0, count - 1, lap, so_far)


MOST = 2048


def shifted(block, axis, distance):
    count = lax.axis_size(axis)
    return lax.ppermute(block, axis, [(i, (i + distance) % count) for i in range(count)])


def tp_layout():
    count = lax.axis_size("tp")
    inner = 2 if count % 2 == 0 else 1
    return count, inner, count // inner


def tp_pieces(block):
    count, inner, outer = tp_layout()
    inner_rank = lax.axis_index("tp") % inner
    sources = [block]
    if inner == 2:
        sources.append(lax.ppermute(block, "tp", [(i, i ^ 1) for i in range(count)]))
    slots = [[source if step == 0 else shifted(source, "tp", -inner * step) for source in sources]
             for step in range(outer)]
    pieces = []
    for own, *other in slots:
        if inner == 2:
            pieces.append(jnp.where(inner_rank == 0, own, other[0]))
            pieces.append(jnp.where(inner_rank == 0, other[0], own))
        else:
            pieces.append(own)
    return pieces


def tp_assemble(pieces, axis):
    count, inner, outer = tp_layout()
    outer_rank = lax.axis_index("tp") // inner
    width = pieces[0].shape[axis]
    doubled = jnp.concatenate(pieces + pieces, axis=axis)
    start = ((count - inner * outer_rank) % count) * width
    return lax.dynamic_slice_in_dim(doubled, start, count * width, axis)


def tp_gather(block, axis):
    return tp_assemble(tp_pieces(block), axis)


def tp_scatter(values, send_dtype):
    count, inner, outer = tp_layout()
    rank = lax.axis_index("tp")
    outer_rank, inner_rank = rank // inner, rank % inner
    width = values.shape[1] // count
    span = inner * width
    total = lax.dynamic_slice_in_dim(values, outer_rank * span, span, 1).astype(jnp.float32)
    for step in range(1, outer):
        piece = lax.dynamic_slice_in_dim(values, ((outer_rank + step) % outer) * span, span, 1)
        total = total + shifted(piece.astype(send_dtype), "tp", inner * step).astype(jnp.float32)
    mine = lax.dynamic_slice_in_dim(total, inner_rank * width, width, 1)
    if inner == 2:
        theirs = lax.dynamic_slice_in_dim(total, (1 - inner_rank) * width, width, 1)
        swapped = lax.ppermute(theirs.astype(send_dtype), "tp", [(i, i ^ 1) for i in range(count)])
        mine = mine + swapped.astype(jnp.float32)
    return mine


def carried_in_scan(through, state, reach):
    heads = through.shape[0]

    def pack(decay, value):
        return jnp.concatenate([value.reshape(-1), decay])

    def unpack(packed):
        return (packed[-heads:], packed[:-heads].reshape(state.shape))

    rank = lax.axis_index("req")
    neutral = pack(jnp.ones_like(through), jnp.zeros_like(state))
    carry = jnp.where(rank >= 1, from_behind(pack(through, state), "req", 1), neutral)
    distance = 1
    while distance < reach:
        prev = from_behind(carry, "req", distance)
        joined = pack(*combine_states(unpack(prev), unpack(carry)))
        carry = jnp.where(rank >= distance, joined, carry)
        distance *= 2
    return unpack(carry)[1]


def rms_rows(values, gain):
    values = values.astype(jnp.float32)
    factor = lax.rsqrt(jnp.mean(values * values, axis=-1, keepdims=True) + epsilon)
    return values * factor * gain


def positions_of(seg_all):
    total_rows = seg_all.shape[0]
    indices = jnp.arange(total_rows, dtype=jnp.int32)
    begins = jnp.concatenate([jnp.ones((1,), dtype=bool), seg_all[1:] != seg_all[:-1]])
    first_index = lax.cummax(jnp.where(begins, indices, jnp.zeros_like(indices)), axis=0)
    return indices - first_index


def rotate(values, places):
    half_dim = values.shape[-1] // 2
    freqs = jnp.exp(-jnp.log(10000.0) * jnp.arange(half_dim, dtype=jnp.float32) / half_dim)
    angles = places.astype(jnp.float32)[:, None] * freqs[None, :]
    cosine = jnp.cos(angles)[:, None, :]
    sine = jnp.sin(angles)[:, None, :]
    first_half = values[..., :half_dim]
    second_half = values[..., half_dim:]
    return jnp.concatenate(
        [first_half * cosine - second_half * sine, second_half * cosine + first_half * sine],
        axis=-1,
    )


def conv_rows(extended, seg_extended, kernel, seg_now):
    kernel_len = kernel.shape[0]
    rows_out = seg_now.shape[0]
    result = jnp.zeros((rows_out, extended.shape[1]), jnp.float32)
    for offset in range(kernel_len):
        window_rows = extended[offset : offset + rows_out]
        matches = (seg_extended[offset : offset + rows_out] == seg_now)[:, None]
        result = result + jnp.where(matches, window_rows * kernel[offset][None, :], 0.0)
    return jax.nn.silu(result)


def ssd_block(
    inner, write_rows, read_rows, steps_dt, log_decay, seg_block, seg_before, state_prev, skip_gain
):
    length = inner.shape[0]
    cumul = jnp.cumsum(log_decay, axis=0)
    order = jnp.arange(length, dtype=jnp.int32)
    within = (seg_block[:, None] == seg_block[None, :]) & (order[:, None] >= order[None, :])
    spread = cumul.T[:, :, None] - cumul.T[:, None, :]
    decays = jnp.where(within[None], jnp.exp(jnp.minimum(spread, 0.0)), 0.0)
    intersection = jnp.dot(read_rows, write_rows.T, precision=highest)
    mixing = decays * intersection[None] * steps_dt.T[:, None, :]
    local_out = jnp.einsum("hts,shp->thp", mixing, inner, precision=highest)
    carried = jnp.where((seg_block == seg_before)[:, None], jnp.exp(cumul), 0.0)
    from_state = jnp.einsum("tn,hpn->thp", read_rows, state_prev, precision=highest)
    outputs = local_out + carried[:, :, None] * from_state + skip_gain[None, :, None] * inner
    tail_weight = (
        jnp.where((seg_block == seg_block[-1])[:, None], jnp.exp(cumul[-1][None, :] - cumul), 0.0)
        * steps_dt
    )
    keep_factor = jnp.where(seg_block[-1] == seg_before, jnp.exp(cumul[-1]), 0.0)
    state_next = keep_factor[:, None, None] * state_prev + jnp.einsum(
        "sh,shp,sn->hpn", tail_weight, inner, write_rows, precision=highest
    )
    return (outputs, state_next)


def accumulate_rows(left_rows, weight_rows):
    return jnp.dot(left_rows, weight_rows, preferred_element_type=jnp.float32)


def combine_states(earlier, later):
    return (earlier[0] * later[0], later[0][:, None, None] * earlier[1] + later[1])


def on_device(
    hidden_in,
    embeds,
    seg_ids,
    mamba_gain,
    w_z,
    w_x,
    w_bc,
    w_dt,
    dt_bias,
    decay_rate,
    conv_x,
    conv_bc,
    skip_gain,
    gate_gain,
    w_out,
    attn_gain,
    w_qkv,
    adapter_down,
    adapter_up,
    w_o,
):
    rows_here = hidden_in.shape[0]
    tensor_size = lax.axis_size("tp")
    req_rank = lax.axis_index("req")
    first_row = req_rank * rows_here
    paired = tp_pieces(jnp.stack([hidden_in, w_bc]))
    full_hidden = tp_assemble([piece[0] for piece in paired], 1)
    full_w_bc = tp_assemble([piece[1] for piece in paired], 0)
    full_embeds = tp_gather(embeds, 1)
    normed = rms_rows(full_hidden, mamba_gain).astype(jnp.bfloat16)
    gate_z = jnp.dot(normed, w_z, preferred_element_type=jnp.float32)
    inner_x = jnp.dot(normed, w_x, preferred_element_type=jnp.float32)
    raw_dt = jnp.dot(normed, w_dt, preferred_element_type=jnp.float32)
    state_io = accumulate_rows(normed, full_w_bc)
    mixed_in = jnp.concatenate([inner_x, state_io], axis=1)
    kernel_len = conv_x.shape[0]
    tail_rows = mixed_in[rows_here - (kernel_len - 1) :]
    prior_rows = from_behind(tail_rows, "req", 1)
    extended = jnp.concatenate([prior_rows, mixed_in], axis=0)
    seg_padded = jnp.concatenate(
        [jnp.full((kernel_len - 1,), -1, dtype=jnp.int32), seg_ids], axis=0
    )
    seg_extended = lax.dynamic_slice_in_dim(seg_padded, first_row, rows_here + kernel_len - 1, 0)
    seg_now = lax.dynamic_slice_in_dim(seg_ids, first_row, rows_here, 0)
    kernel = jnp.concatenate([conv_x, conv_bc], axis=1)
    conv_out = conv_rows(extended, seg_extended, kernel, seg_now)
    inner_here = w_z.shape[1]
    heads_here = w_dt.shape[1]
    head_dim = inner_here // heads_here
    state_dim = state_io.shape[1] // 2
    inner_c = conv_out[:, :inner_here].reshape(rows_here, heads_here, head_dim)
    write_rows = conv_out[:, inner_here : inner_here + state_dim]
    read_rows = conv_out[:, inner_here + state_dim :]
    steps_dt = jax.nn.softplus(raw_dt + dt_bias)
    log_decay = -steps_dt * decay_rate
    seg_before = jnp.where(req_rank > 0, seg_ids[jnp.maximum(first_row - 1, 0)], -1)
    seg_prior = jnp.concatenate([seg_before[None], seg_now[:-1]], axis=0)
    block_rows = math.gcd(rows_here, 256)
    count_blocks = rows_here // block_rows
    block_before = seg_prior.reshape(count_blocks, block_rows)[:, 0]

    def ssd_step(state_prev, pieces):
        blk_inner, blk_write, blk_read, blk_dt, blk_decay, blk_seg, blk_before = pieces
        outputs, state_next = ssd_block(
            blk_inner,
            blk_write,
            blk_read,
            blk_dt,
            blk_decay,
            blk_seg,
            blk_before,
            state_prev,
            skip_gain,
        )
        return (state_next, outputs)

    zero_state = jnp.zeros((heads_here, head_dim, state_dim), jnp.float32)
    local_state, local_out = lax.scan(
        ssd_step,
        zero_state,
        (
            inner_c.reshape(count_blocks, block_rows, heads_here, head_dim),
            write_rows.reshape(count_blocks, block_rows, state_dim),
            read_rows.reshape(count_blocks, block_rows, state_dim),
            steps_dt.reshape(count_blocks, block_rows, heads_here),
            log_decay.reshape(count_blocks, block_rows, heads_here),
            seg_now.reshape(count_blocks, block_rows),
            block_before,
        ),
    )
    local_out = local_out.reshape(rows_here, heads_here, head_dim)
    cumul_all = jnp.cumsum(log_decay, axis=0)
    through = jnp.where(seg_now[-1] == seg_before, jnp.exp(cumul_all[-1]), 0.0)
    carried_in = carried_in_scan(through, local_state, -(-MOST // rows_here))
    carried = jnp.where((seg_now == seg_before)[:, None], jnp.exp(cumul_all), 0.0)
    from_state = jnp.einsum("tn,hpn->thp", read_rows, carried_in, precision=highest)
    ssm_y = local_out + carried[:, :, None] * from_state
    final_state = local_state + through[:, None, None] * carried_in
    gated_rows = ssm_y.reshape(rows_here, inner_here) * jax.nn.silu(gate_z)
    square_part = jnp.sum(gated_rows * gated_rows, axis=1)
    gained = (gated_rows * gate_gain).astype(jnp.bfloat16)
    mix_terms = jnp.dot(gained, w_out, preferred_element_type=jnp.float32)
    with_squares = jnp.concatenate([mix_terms, jnp.tile(square_part[None], (1, tensor_size))], axis=0)
    reduced = tp_scatter(with_squares, jnp.float32)
    factor = lax.rsqrt(reduced[rows_here] / (inner_here * tensor_size) + epsilon)
    mix_share = reduced[:rows_here] * factor[:, None]
    mid_here = (hidden_in.astype(jnp.float32) + mix_share).astype(jnp.bfloat16)
    mid_full = tp_gather(mid_here, 1)
    joined = jnp.concatenate([mid_full, full_embeds], axis=1)
    attn_in = rms_rows(joined, attn_gain).astype(jnp.bfloat16)
    low_sum = accumulate_rows(attn_in, tp_gather(adapter_down, 0))
    low_rank = low_sum.astype(jnp.bfloat16)
    rank_cols = adapter_up.shape[1]
    cols_here = w_qkv.shape[2]
    heads_attn = cols_here // AHD
    projected = jnp.dot(
        attn_in, w_qkv.reshape(w_qkv.shape[0], 3 * cols_here), preferred_element_type=jnp.float32
    ).reshape(rows_here, 3, cols_here)
    projected = projected + jnp.einsum(
        "tjr,jrc->tjc",
        low_rank.reshape(rows_here, 3, rank_cols),
        adapter_up,
        preferred_element_type=jnp.float32,
    )
    places = lax.dynamic_slice_in_dim(positions_of(seg_ids), first_row, rows_here, 0)
    queries = rotate(projected[:, 0].reshape(rows_here, heads_attn, AHD), places).astype(
        jnp.bfloat16
    )
    key_rows = rotate(projected[:, 1].reshape(rows_here, heads_attn, AHD), places).astype(
        jnp.bfloat16
    )
    value_rows = projected[:, 2].astype(jnp.bfloat16)
    kv_pair = jnp.stack([key_rows.reshape(rows_here, cols_here), value_rows], axis=1)
    query_index = first_row + jnp.arange(rows_here, dtype=jnp.int32)
    inv_root = 1.0 / math.sqrt(AHD)

    def absorb(running, block_kv, first_key):
        row_top, denom_sum, weighted = running
        key_count = block_kv.shape[0]
        key_index = first_key + jnp.arange(key_count, dtype=jnp.int32)
        key_seg = lax.dynamic_slice_in_dim(seg_ids, jnp.maximum(first_key, 0), key_count, 0)
        allowed = (
            (key_seg[None, :] == seg_now[:, None])
            & (key_index[None, :] <= query_index[:, None])
            & (key_index[None, :] >= 0)
        )
        block_keys = block_kv[:, 0].reshape(key_count, heads_attn, AHD)
        block_vals = block_kv[:, 1].reshape(key_count, heads_attn, AHD)
        scores = (
            jnp.einsum("qhe,khe->hqk", queries, block_keys, preferred_element_type=jnp.float32)
            * inv_root
        )
        masked = jnp.where(allowed[None], scores, -1e30)
        new_top = jnp.maximum(row_top, jnp.max(masked, axis=-1))
        weights = jnp.where(allowed[None], jnp.exp(scores - new_top[:, :, None]), 0.0)
        shrink = jnp.exp(row_top - new_top)
        denom_sum = denom_sum * shrink + jnp.sum(weights, axis=-1)
        weighted = weighted * shrink[:, :, None] + jnp.einsum(
            "hqk,khe->hqe",
            weights.astype(jnp.bfloat16),
            block_vals,
            preferred_element_type=jnp.float32,
        )
        return (new_top, denom_sum, weighted)

    start_state = (
        jnp.full((heads_attn, rows_here), -1e30, jnp.float32),
        jnp.zeros((heads_attn, rows_here), jnp.float32),
        jnp.zeros((heads_attn, rows_here, AHD), jnp.float32),
    )
    reach_hops = min(lax.axis_size("req") - 1, -(-(MOST - 1) // rows_here))
    running = absorb(start_state, kv_pair, first_row)
    for hop_count in range(1, reach_hops + 1):
        moving = from_behind(kv_pair, "req", hop_count)
        running = absorb(running, moving, first_row - hop_count * rows_here)
    row_top, denom_sum, weighted = running
    attended = (weighted / denom_sum[:, :, None]).astype(jnp.bfloat16)
    attended = attended.transpose(1, 0, 2).reshape(rows_here, cols_here)
    attn_terms = jnp.dot(attended, w_o, preferred_element_type=jnp.float32)
    attn_share = tp_scatter(attn_terms, jnp.bfloat16)
    hidden_out = (mid_here.astype(jnp.float32) + attn_share).astype(jnp.bfloat16)
    return (hidden_out, final_state[None], kv_pair)


def solution(mesh):
    in_specs = (
        P("req", "tp"),
        P("req", "tp"),
        P(),
        P(),
        P(None, "tp"),
        P(None, "tp"),
        P("tp", None),
        P(None, "tp"),
        P("tp"),
        P("tp"),
        P(None, "tp"),
        P(),
        P("tp"),
        P("tp"),
        P("tp", None),
        P(),
        P(None, None, "tp"),
        P("tp", None),
        P(None, None, "tp"),
        P("tp", None),
    )
    out_specs = (P("req", "tp"), P("req", "tp", None, None), P("req", None, "tp"))
    return jax.shard_map(
        on_device, mesh=mesh, in_specs=in_specs, out_specs=out_specs, check_vma=False
    )
```

```python
import math

import jax
import jax.numpy as jnp
from jax import lax
from jax.sharding import PartitionSpec as P

AHD = 128


highest = lax.Precision.HIGHEST
epsilon = 1e-05


def from_behind(block, axis, distance):
    devices = range(lax.axis_size(axis))
    route = [(i - distance, i) for i in devices if i - distance in devices]
    return lax.ppermute(block, axis, route)


def carried_in_2(value, axis, join, neutral):
    count, mine = (lax.axis_size(axis), lax.axis_index(axis))
    pieces = jax.tree.map(lambda part: lax.all_gather(part, axis), value)
    so_far = jax.tree.map(
        lambda part, zero: jnp.full_like(part, 0) + jnp.asarray(zero, part.dtype), value, neutral
    )

    def lap(position, so_far):
        longer = join(so_far, jax.tree.map(lambda part: part[position], pieces))
        return jax.tree.map(lambda new, old: jnp.where(position < mine, new, old), longer, so_far)

    return lax.fori_loop(0, count - 1, lap, so_far)


MOST = 2048


def shifted(block, axis, distance):
    count = lax.axis_size(axis)
    return lax.ppermute(block, axis, [(i, (i + distance) % count) for i in range(count)])


def tp_layout():
    count = lax.axis_size("tp")
    inner = 2 if count % 2 == 0 else 1
    return count, inner, count // inner


def tp_pieces(block):
    count, inner, outer = tp_layout()
    inner_rank = lax.axis_index("tp") % inner
    sources = [block]
    if inner == 2:
        sources.append(lax.ppermute(block, "tp", [(i, i ^ 1) for i in range(count)]))
    slots = [[source if step == 0 else shifted(source, "tp", -inner * step) for source in sources]
             for step in range(outer)]
    pieces = []
    for own, *other in slots:
        if inner == 2:
            pieces.append(jnp.where(inner_rank == 0, own, other[0]))
            pieces.append(jnp.where(inner_rank == 0, other[0], own))
        else:
            pieces.append(own)
    return pieces


def tp_assemble(pieces, axis):
    count, inner, outer = tp_layout()
    outer_rank = lax.axis_index("tp") // inner
    width = pieces[0].shape[axis]
    doubled = jnp.concatenate(pieces + pieces, axis=axis)
    start = ((count - inner * outer_rank) % count) * width
    return lax.dynamic_slice_in_dim(doubled, start, count * width, axis)


def tp_gather(block, axis):
    return tp_assemble(tp_pieces(block), axis)


def tp_scatter(values, send_dtype):
    count, inner, outer = tp_layout()
    rank = lax.axis_index("tp")
    outer_rank, inner_rank = rank // inner, rank % inner
    width = values.shape[1] // count
    span = inner * width
    total = lax.dynamic_slice_in_dim(values, outer_rank * span, span, 1).astype(jnp.float32)
    for step in range(1, outer):
        piece = lax.dynamic_slice_in_dim(values, ((outer_rank + step) % outer) * span, span, 1)
        total = total + shifted(piece.astype(send_dtype), "tp", inner * step).astype(jnp.float32)
    mine = lax.dynamic_slice_in_dim(total, inner_rank * width, width, 1)
    if inner == 2:
        theirs = lax.dynamic_slice_in_dim(total, (1 - inner_rank) * width, width, 1)
        swapped = lax.ppermute(theirs.astype(send_dtype), "tp", [(i, i ^ 1) for i in range(count)])
        mine = mine + swapped.astype(jnp.float32)
    return mine


def carried_in_scan(through, state, reach):
    heads = through.shape[0]

    def pack(decay, value):
        return jnp.concatenate([value.reshape(-1), decay])

    def unpack(packed):
        return (packed[-heads:], packed[:-heads].reshape(state.shape))

    rank = lax.axis_index("req")
    neutral = pack(jnp.ones_like(through), jnp.zeros_like(state))
    carry = jnp.where(rank >= 1, from_behind(pack(through, state), "req", 1), neutral)
    distance = 1
    while distance < reach:
        prev = from_behind(carry, "req", distance)
        joined = pack(*combine_states(unpack(prev), unpack(carry)))
        carry = jnp.where(rank >= distance, joined, carry)
        distance *= 2
    return unpack(carry)[1]


def rms_rows(values, gain):
    values = values.astype(jnp.float32)
    factor = lax.rsqrt(jnp.mean(values * values, axis=-1, keepdims=True) + epsilon)
    return values * factor * gain


def positions_of(seg_all):
    total_rows = seg_all.shape[0]
    indices = jnp.arange(total_rows, dtype=jnp.int32)
    begins = jnp.concatenate([jnp.ones((1,), dtype=bool), seg_all[1:] != seg_all[:-1]])
    first_index = lax.cummax(jnp.where(begins, indices, jnp.zeros_like(indices)), axis=0)
    return indices - first_index


def rotate(values, places):
    half_dim = values.shape[-1] // 2
    freqs = jnp.exp(-jnp.log(10000.0) * jnp.arange(half_dim, dtype=jnp.float32) / half_dim)
    angles = places.astype(jnp.float32)[:, None] * freqs[None, :]
    cosine = jnp.cos(angles)[:, None, :]
    sine = jnp.sin(angles)[:, None, :]
    first_half = values[..., :half_dim]
    second_half = values[..., half_dim:]
    return jnp.concatenate(
        [first_half * cosine - second_half * sine, second_half * cosine + first_half * sine],
        axis=-1,
    )


def conv_rows(extended, seg_extended, kernel, seg_now):
    kernel_len = kernel.shape[0]
    rows_out = seg_now.shape[0]
    result = jnp.zeros((rows_out, extended.shape[1]), jnp.float32)
    for offset in range(kernel_len):
        window_rows = extended[offset : offset + rows_out]
        matches = (seg_extended[offset : offset + rows_out] == seg_now)[:, None]
        result = result + jnp.where(matches, window_rows * kernel[offset][None, :], 0.0)
    return jax.nn.silu(result)


def ssd_block(
    inner, write_rows, read_rows, steps_dt, log_decay, seg_block, seg_before, state_prev, skip_gain
):
    length = inner.shape[0]
    cumul = jnp.cumsum(log_decay, axis=0)
    order = jnp.arange(length, dtype=jnp.int32)
    within = (seg_block[:, None] == seg_block[None, :]) & (order[:, None] >= order[None, :])
    spread = cumul.T[:, :, None] - cumul.T[:, None, :]
    decays = jnp.where(within[None], jnp.exp(jnp.minimum(spread, 0.0)), 0.0)
    intersection = jnp.dot(read_rows, write_rows.T, precision=highest)
    mixing = decays * intersection[None] * steps_dt.T[:, None, :]
    local_out = jnp.einsum("hts,shp->thp", mixing, inner, precision=highest)
    carried = jnp.where((seg_block == seg_before)[:, None], jnp.exp(cumul), 0.0)
    from_state = jnp.einsum("tn,hpn->thp", read_rows, state_prev, precision=highest)
    outputs = local_out + carried[:, :, None] * from_state + skip_gain[None, :, None] * inner
    tail_weight = (
        jnp.where((seg_block == seg_block[-1])[:, None], jnp.exp(cumul[-1][None, :] - cumul), 0.0)
        * steps_dt
    )
    keep_factor = jnp.where(seg_block[-1] == seg_before, jnp.exp(cumul[-1]), 0.0)
    state_next = keep_factor[:, None, None] * state_prev + jnp.einsum(
        "sh,shp,sn->hpn", tail_weight, inner, write_rows, precision=highest
    )
    return (outputs, state_next)


def accumulate_rows(left_rows, weight_rows):
    return jnp.dot(left_rows, weight_rows, preferred_element_type=jnp.float32)


def combine_states(earlier, later):
    return (earlier[0] * later[0], later[0][:, None, None] * earlier[1] + later[1])


def on_device(
    hidden_in,
    embeds,
    seg_ids,
    mamba_gain,
    w_z,
    w_x,
    w_bc,
    w_dt,
    dt_bias,
    decay_rate,
    conv_x,
    conv_bc,
    skip_gain,
    gate_gain,
    w_out,
    attn_gain,
    w_qkv,
    adapter_down,
    adapter_up,
    w_o,
):
    rows_here = hidden_in.shape[0]
    tensor_size = lax.axis_size("tp")
    req_rank = lax.axis_index("req")
    first_row = req_rank * rows_here
    paired = tp_pieces(jnp.stack([hidden_in, w_bc]))
    full_hidden = tp_assemble([piece[0] for piece in paired], 1)
    full_w_bc = tp_assemble([piece[1] for piece in paired], 0)
    normed = rms_rows(full_hidden, mamba_gain).astype(jnp.bfloat16)
    normed, embeds, adapter_down = lax.optimization_barrier((normed, embeds, adapter_down))
    full_embeds = tp_gather(embeds, 1)
    full_down = tp_gather(adapter_down, 0)
    gate_z = jnp.dot(normed, w_z, preferred_element_type=jnp.float32)
    inner_x = jnp.dot(normed, w_x, preferred_element_type=jnp.float32)
    raw_dt = jnp.dot(normed, w_dt, preferred_element_type=jnp.float32)
    state_io = accumulate_rows(normed, full_w_bc)
    mixed_in = jnp.concatenate([inner_x, state_io], axis=1)
    kernel_len = conv_x.shape[0]
    tail_rows = mixed_in[rows_here - (kernel_len - 1) :]
    prior_rows = from_behind(tail_rows, "req", 1)
    extended = jnp.concatenate([prior_rows, mixed_in], axis=0)
    seg_padded = jnp.concatenate(
        [jnp.full((kernel_len - 1,), -1, dtype=jnp.int32), seg_ids], axis=0
    )
    seg_extended = lax.dynamic_slice_in_dim(seg_padded, first_row, rows_here + kernel_len - 1, 0)
    seg_now = lax.dynamic_slice_in_dim(seg_ids, first_row, rows_here, 0)
    kernel = jnp.concatenate([conv_x, conv_bc], axis=1)
    conv_out = conv_rows(extended, seg_extended, kernel, seg_now)
    inner_here = w_z.shape[1]
    heads_here = w_dt.shape[1]
    head_dim = inner_here // heads_here
    state_dim = state_io.shape[1] // 2
    inner_c = conv_out[:, :inner_here].reshape(rows_here, heads_here, head_dim)
    write_rows = conv_out[:, inner_here : inner_here + state_dim]
    read_rows = conv_out[:, inner_here + state_dim :]
    steps_dt = jax.nn.softplus(raw_dt + dt_bias)
    log_decay = -steps_dt * decay_rate
    seg_before = jnp.where(req_rank > 0, seg_ids[jnp.maximum(first_row - 1, 0)], -1)
    seg_prior = jnp.concatenate([seg_before[None], seg_now[:-1]], axis=0)
    block_rows = math.gcd(rows_here, 256)
    count_blocks = rows_here // block_rows
    block_before = seg_prior.reshape(count_blocks, block_rows)[:, 0]

    def ssd_step(state_prev, pieces):
        blk_inner, blk_write, blk_read, blk_dt, blk_decay, blk_seg, blk_before = pieces
        outputs, state_next = ssd_block(
            blk_inner,
            blk_write,
            blk_read,
            blk_dt,
            blk_decay,
            blk_seg,
            blk_before,
            state_prev,
            skip_gain,
        )
        return (state_next, outputs)

    zero_state = jnp.zeros((heads_here, head_dim, state_dim), jnp.float32)
    local_state, local_out = lax.scan(
        ssd_step,
        zero_state,
        (
            inner_c.reshape(count_blocks, block_rows, heads_here, head_dim),
            write_rows.reshape(count_blocks, block_rows, state_dim),
            read_rows.reshape(count_blocks, block_rows, state_dim),
            steps_dt.reshape(count_blocks, block_rows, heads_here),
            log_decay.reshape(count_blocks, block_rows, heads_here),
            seg_now.reshape(count_blocks, block_rows),
            block_before,
        ),
    )
    local_out = local_out.reshape(rows_here, heads_here, head_dim)
    cumul_all = jnp.cumsum(log_decay, axis=0)
    through = jnp.where(seg_now[-1] == seg_before, jnp.exp(cumul_all[-1]), 0.0)
    carried_in = carried_in_scan(through, local_state, -(-MOST // rows_here))
    carried = jnp.where((seg_now == seg_before)[:, None], jnp.exp(cumul_all), 0.0)
    from_state = jnp.einsum("tn,hpn->thp", read_rows, carried_in, precision=highest)
    ssm_y = local_out + carried[:, :, None] * from_state
    final_state = local_state + through[:, None, None] * carried_in
    gated_rows = ssm_y.reshape(rows_here, inner_here) * jax.nn.silu(gate_z)
    square_part = jnp.sum(gated_rows * gated_rows, axis=1)
    gained = (gated_rows * gate_gain).astype(jnp.bfloat16)
    mix_terms = jnp.dot(gained, w_out, preferred_element_type=jnp.float32)
    with_squares = jnp.concatenate([mix_terms, jnp.tile(square_part[None], (1, tensor_size))], axis=0)
    reduced = tp_scatter(with_squares, jnp.bfloat16)
    factor = lax.rsqrt(reduced[rows_here] / (inner_here * tensor_size) + epsilon)
    mix_share = reduced[:rows_here] * factor[:, None]
    mid_here = (hidden_in.astype(jnp.float32) + mix_share).astype(jnp.bfloat16)
    mid_full = tp_gather(mid_here, 1)
    joined = jnp.concatenate([mid_full, full_embeds], axis=1)
    attn_in = rms_rows(joined, attn_gain).astype(jnp.bfloat16)
    low_sum = accumulate_rows(attn_in, full_down)
    low_rank = low_sum.astype(jnp.bfloat16)
    rank_cols = adapter_up.shape[1]
    cols_here = w_qkv.shape[2]
    heads_attn = cols_here // AHD
    projected = jnp.dot(
        attn_in, w_qkv.reshape(w_qkv.shape[0], 3 * cols_here), preferred_element_type=jnp.float32
    ).reshape(rows_here, 3, cols_here)
    projected = projected + jnp.einsum(
        "tjr,jrc->tjc",
        low_rank.reshape(rows_here, 3, rank_cols),
        adapter_up,
        preferred_element_type=jnp.float32,
    )
    places = lax.dynamic_slice_in_dim(positions_of(seg_ids), first_row, rows_here, 0)
    queries = rotate(projected[:, 0].reshape(rows_here, heads_attn, AHD), places).astype(
        jnp.bfloat16
    )
    key_rows = rotate(projected[:, 1].reshape(rows_here, heads_attn, AHD), places).astype(
        jnp.bfloat16
    )
    value_rows = projected[:, 2].astype(jnp.bfloat16)
    kv_pair = jnp.stack([key_rows.reshape(rows_here, cols_here), value_rows], axis=1)
    query_index = first_row + jnp.arange(rows_here, dtype=jnp.int32)
    inv_root = 1.0 / math.sqrt(AHD)

    def absorb(running, block_kv, first_key):
        row_top, denom_sum, weighted = running
        key_count = block_kv.shape[0]
        key_index = first_key + jnp.arange(key_count, dtype=jnp.int32)
        key_seg = lax.dynamic_slice_in_dim(seg_ids, jnp.maximum(first_key, 0), key_count, 0)
        allowed = (
            (key_seg[None, :] == seg_now[:, None])
            & (key_index[None, :] <= query_index[:, None])
            & (key_index[None, :] >= 0)
        )
        block_keys = block_kv[:, 0].reshape(key_count, heads_attn, AHD)
        block_vals = block_kv[:, 1].reshape(key_count, heads_attn, AHD)
        scores = (
            jnp.einsum("qhe,khe->hqk", queries, block_keys, preferred_element_type=jnp.float32)
            * inv_root
        )
        masked = jnp.where(allowed[None], scores, -1e30)
        new_top = jnp.maximum(row_top, jnp.max(masked, axis=-1))
        weights = jnp.where(allowed[None], jnp.exp(scores - new_top[:, :, None]), 0.0)
        shrink = jnp.exp(row_top - new_top)
        denom_sum = denom_sum * shrink + jnp.sum(weights, axis=-1)
        weighted = weighted * shrink[:, :, None] + jnp.einsum(
            "hqk,khe->hqe",
            weights.astype(jnp.bfloat16),
            block_vals,
            preferred_element_type=jnp.float32,
        )
        return (new_top, denom_sum, weighted)

    start_state = (
        jnp.full((heads_attn, rows_here), -1e30, jnp.float32),
        jnp.zeros((heads_attn, rows_here), jnp.float32),
        jnp.zeros((heads_attn, rows_here, AHD), jnp.float32),
    )
    reach_hops = min(lax.axis_size("req") - 1, -(-(MOST - 1) // rows_here))
    running = absorb(start_state, kv_pair, first_row)
    for hop_count in range(1, reach_hops + 1):
        moving = from_behind(kv_pair, "req", hop_count)
        running = absorb(running, moving, first_row - hop_count * rows_here)
    row_top, denom_sum, weighted = running
    attended = (weighted / denom_sum[:, :, None]).astype(jnp.bfloat16)
    attended = attended.transpose(1, 0, 2).reshape(rows_here, cols_here)
    attn_terms = jnp.dot(attended, w_o, preferred_element_type=jnp.float32)
    attn_share = tp_scatter(attn_terms, jnp.bfloat16)
    hidden_out = (mid_here.astype(jnp.float32) + attn_share).astype(jnp.bfloat16)
    return (hidden_out, final_state[None], kv_pair)


def solution(mesh):
    in_specs = (
        P("req", "tp"),
        P("req", "tp"),
        P(),
        P(),
        P(None, "tp"),
        P(None, "tp"),
        P("tp", None),
        P(None, "tp"),
        P("tp"),
        P("tp"),
        P(None, "tp"),
        P(),
        P("tp"),
        P("tp"),
        P("tp", None),
        P(),
        P(None, None, "tp"),
        P("tp", None),
        P(None, None, "tp"),
        P("tp", None),
    )
    out_specs = (P("req", "tp"), P("req", "tp", None, None), P("req", None, "tp"))
    return jax.shard_map(
        on_device, mesh=mesh, in_specs=in_specs, out_specs=out_specs, check_vma=False
    )
```

```python
import math

import jax
import jax.numpy as jnp
from jax import lax
from jax.sharding import PartitionSpec as P

AHD = 128


highest = lax.Precision.HIGHEST
epsilon = 1e-05


def from_behind(block, axis, distance):
    devices = range(lax.axis_size(axis))
    route = [(i - distance, i) for i in devices if i - distance in devices]
    return lax.ppermute(block, axis, route)


def carried_in_2(value, axis, join, neutral):
    count, mine = (lax.axis_size(axis), lax.axis_index(axis))
    pieces = jax.tree.map(lambda part: lax.all_gather(part, axis), value)
    so_far = jax.tree.map(
        lambda part, zero: jnp.full_like(part, 0) + jnp.asarray(zero, part.dtype), value, neutral
    )

    def lap(position, so_far):
        longer = join(so_far, jax.tree.map(lambda part: part[position], pieces))
        return jax.tree.map(lambda new, old: jnp.where(position < mine, new, old), longer, so_far)

    return lax.fori_loop(0, count - 1, lap, so_far)


MOST = 2048


def shifted(block, axis, distance):
    count = lax.axis_size(axis)
    return lax.ppermute(block, axis, [(i, (i + distance) % count) for i in range(count)])


def tp_layout():
    count = lax.axis_size("tp")
    inner = 2 if count % 2 == 0 else 1
    return count, inner, count // inner


def tp_pieces(block):
    count, inner, outer = tp_layout()
    inner_rank = lax.axis_index("tp") % inner
    sources = [block]
    if inner == 2:
        sources.append(lax.ppermute(block, "tp", [(i, i ^ 1) for i in range(count)]))
    slots = [[source if step == 0 else shifted(source, "tp", -inner * step) for source in sources]
             for step in range(outer)]
    pieces = []
    for own, *other in slots:
        if inner == 2:
            pieces.append(jnp.where(inner_rank == 0, own, other[0]))
            pieces.append(jnp.where(inner_rank == 0, other[0], own))
        else:
            pieces.append(own)
    return pieces


def tp_assemble(pieces, axis):
    count, inner, outer = tp_layout()
    outer_rank = lax.axis_index("tp") // inner
    width = pieces[0].shape[axis]
    doubled = jnp.concatenate(pieces + pieces, axis=axis)
    start = ((count - inner * outer_rank) % count) * width
    return lax.dynamic_slice_in_dim(doubled, start, count * width, axis)


def tp_gather(block, axis):
    return tp_assemble(tp_pieces(block), axis)


def tp_scatter(values, send_dtype):
    count, inner, outer = tp_layout()
    rank = lax.axis_index("tp")
    outer_rank, inner_rank = rank // inner, rank % inner
    width = values.shape[1] // count
    span = inner * width
    total = lax.dynamic_slice_in_dim(values, outer_rank * span, span, 1).astype(jnp.float32)
    for step in range(1, outer):
        piece = lax.dynamic_slice_in_dim(values, ((outer_rank + step) % outer) * span, span, 1)
        total = total + shifted(piece.astype(send_dtype), "tp", inner * step).astype(jnp.float32)
    mine = lax.dynamic_slice_in_dim(total, inner_rank * width, width, 1)
    if inner == 2:
        theirs = lax.dynamic_slice_in_dim(total, (1 - inner_rank) * width, width, 1)
        swapped = lax.ppermute(theirs.astype(send_dtype), "tp", [(i, i ^ 1) for i in range(count)])
        mine = mine + swapped.astype(jnp.float32)
    return mine


def carried_in_scan(through, state, reach):
    heads = through.shape[0]

    def pack(decay, value):
        return jnp.concatenate([value.reshape(-1), decay])

    def unpack(packed):
        return (packed[-heads:], packed[:-heads].reshape(state.shape))

    rank = lax.axis_index("req")
    neutral = pack(jnp.ones_like(through), jnp.zeros_like(state))

    def earlier(packed, distance):
        return jnp.where(rank >= distance, from_behind(packed, "req", distance), neutral)

    def joined(parts):
        total = parts[0]
        for part in parts[1:]:
            total = pack(*combine_states(unpack(total), unpack(part)))
        return total

    group = min(2, reach)
    mine = pack(through, state)
    near = joined([earlier(mine, distance) for distance in range(group, 0, -1)])
    rounds = -(-reach // group)
    far = [earlier(near, group * step) for step in range(rounds - 1, 0, -1)]
    return unpack(joined(far + [near]))[1]


def rms_rows(values, gain):
    values = values.astype(jnp.float32)
    factor = lax.rsqrt(jnp.mean(values * values, axis=-1, keepdims=True) + epsilon)
    return values * factor * gain


def positions_of(seg_all):
    total_rows = seg_all.shape[0]
    indices = jnp.arange(total_rows, dtype=jnp.int32)
    begins = jnp.concatenate([jnp.ones((1,), dtype=bool), seg_all[1:] != seg_all[:-1]])
    first_index = lax.cummax(jnp.where(begins, indices, jnp.zeros_like(indices)), axis=0)
    return indices - first_index


def rotate(values, places):
    half_dim = values.shape[-1] // 2
    freqs = jnp.exp(-jnp.log(10000.0) * jnp.arange(half_dim, dtype=jnp.float32) / half_dim)
    angles = places.astype(jnp.float32)[:, None] * freqs[None, :]
    cosine = jnp.cos(angles)[:, None, :]
    sine = jnp.sin(angles)[:, None, :]
    first_half = values[..., :half_dim]
    second_half = values[..., half_dim:]
    return jnp.concatenate(
        [first_half * cosine - second_half * sine, second_half * cosine + first_half * sine],
        axis=-1,
    )


def conv_rows(extended, seg_extended, kernel, seg_now):
    kernel_len = kernel.shape[0]
    rows_out = seg_now.shape[0]
    result = jnp.zeros((rows_out, extended.shape[1]), jnp.float32)
    for offset in range(kernel_len):
        window_rows = extended[offset : offset + rows_out]
        matches = (seg_extended[offset : offset + rows_out] == seg_now)[:, None]
        result = result + jnp.where(matches, window_rows * kernel[offset][None, :], 0.0)
    return jax.nn.silu(result)


def ssd_block(
    inner, write_rows, read_rows, steps_dt, log_decay, seg_block, seg_before, state_prev, skip_gain
):
    length = inner.shape[0]
    cumul = jnp.cumsum(log_decay, axis=0)
    order = jnp.arange(length, dtype=jnp.int32)
    within = (seg_block[:, None] == seg_block[None, :]) & (order[:, None] >= order[None, :])
    spread = cumul.T[:, :, None] - cumul.T[:, None, :]
    decays = jnp.where(within[None], jnp.exp(jnp.minimum(spread, 0.0)), 0.0)
    intersection = jnp.dot(read_rows, write_rows.T, precision=highest)
    mixing = decays * intersection[None] * steps_dt.T[:, None, :]
    local_out = jnp.einsum("hts,shp->thp", mixing, inner, precision=highest)
    carried = jnp.where((seg_block == seg_before)[:, None], jnp.exp(cumul), 0.0)
    from_state = jnp.einsum("tn,hpn->thp", read_rows, state_prev, precision=highest)
    outputs = local_out + carried[:, :, None] * from_state + skip_gain[None, :, None] * inner
    tail_weight = (
        jnp.where((seg_block == seg_block[-1])[:, None], jnp.exp(cumul[-1][None, :] - cumul), 0.0)
        * steps_dt
    )
    keep_factor = jnp.where(seg_block[-1] == seg_before, jnp.exp(cumul[-1]), 0.0)
    state_next = keep_factor[:, None, None] * state_prev + jnp.einsum(
        "sh,shp,sn->hpn", tail_weight, inner, write_rows, precision=highest
    )
    return (outputs, state_next)


def accumulate_rows(left_rows, weight_rows):
    return jnp.dot(left_rows, weight_rows, preferred_element_type=jnp.float32)


def combine_states(earlier, later):
    return (earlier[0] * later[0], later[0][:, None, None] * earlier[1] + later[1])


def on_device(
    hidden_in,
    embeds,
    seg_ids,
    mamba_gain,
    w_z,
    w_x,
    w_bc,
    w_dt,
    dt_bias,
    decay_rate,
    conv_x,
    conv_bc,
    skip_gain,
    gate_gain,
    w_out,
    attn_gain,
    w_qkv,
    adapter_down,
    adapter_up,
    w_o,
):
    rows_here = hidden_in.shape[0]
    tensor_size = lax.axis_size("tp")
    req_rank = lax.axis_index("req")
    first_row = req_rank * rows_here
    paired = tp_pieces(jnp.stack([hidden_in, w_bc]))
    full_hidden = tp_assemble([piece[0] for piece in paired], 1)
    full_w_bc = tp_assemble([piece[1] for piece in paired], 0)
    normed = rms_rows(full_hidden, mamba_gain).astype(jnp.bfloat16)
    normed, embeds, adapter_down = lax.optimization_barrier((normed, embeds, adapter_down))
    full_embeds = tp_gather(embeds, 1)
    full_down = tp_gather(adapter_down, 0)
    gate_z = jnp.dot(normed, w_z, preferred_element_type=jnp.float32)
    inner_x = jnp.dot(normed, w_x, preferred_element_type=jnp.float32)
    raw_dt = jnp.dot(normed, w_dt, preferred_element_type=jnp.float32)
    state_io = accumulate_rows(normed, full_w_bc)
    mixed_in = jnp.concatenate([inner_x, state_io], axis=1)
    kernel_len = conv_x.shape[0]
    tail_rows = mixed_in[rows_here - (kernel_len - 1) :]
    prior_rows = from_behind(tail_rows, "req", 1)
    extended = jnp.concatenate([prior_rows, mixed_in], axis=0)
    seg_padded = jnp.concatenate(
        [jnp.full((kernel_len - 1,), -1, dtype=jnp.int32), seg_ids], axis=0
    )
    seg_extended = lax.dynamic_slice_in_dim(seg_padded, first_row, rows_here + kernel_len - 1, 0)
    seg_now = lax.dynamic_slice_in_dim(seg_ids, first_row, rows_here, 0)
    kernel = jnp.concatenate([conv_x, conv_bc], axis=1)
    conv_out = conv_rows(extended, seg_extended, kernel, seg_now)
    inner_here = w_z.shape[1]
    heads_here = w_dt.shape[1]
    head_dim = inner_here // heads_here
    state_dim = state_io.shape[1] // 2
    inner_c = conv_out[:, :inner_here].reshape(rows_here, heads_here, head_dim)
    write_rows = conv_out[:, inner_here : inner_here + state_dim]
    read_rows = conv_out[:, inner_here + state_dim :]
    steps_dt = jax.nn.softplus(raw_dt + dt_bias)
    log_decay = -steps_dt * decay_rate
    seg_before = jnp.where(req_rank > 0, seg_ids[jnp.maximum(first_row - 1, 0)], -1)
    seg_prior = jnp.concatenate([seg_before[None], seg_now[:-1]], axis=0)
    block_rows = math.gcd(rows_here, 256)
    count_blocks = rows_here // block_rows
    block_before = seg_prior.reshape(count_blocks, block_rows)[:, 0]

    def ssd_step(state_prev, pieces):
        blk_inner, blk_write, blk_read, blk_dt, blk_decay, blk_seg, blk_before = pieces
        outputs, state_next = ssd_block(
            blk_inner,
            blk_write,
            blk_read,
            blk_dt,
            blk_decay,
            blk_seg,
            blk_before,
            state_prev,
            skip_gain,
        )
        return (state_next, outputs)

    zero_state = jnp.zeros((heads_here, head_dim, state_dim), jnp.float32)
    local_state, local_out = lax.scan(
        ssd_step,
        zero_state,
        (
            inner_c.reshape(count_blocks, block_rows, heads_here, head_dim),
            write_rows.reshape(count_blocks, block_rows, state_dim),
            read_rows.reshape(count_blocks, block_rows, state_dim),
            steps_dt.reshape(count_blocks, block_rows, heads_here),
            log_decay.reshape(count_blocks, block_rows, heads_here),
            seg_now.reshape(count_blocks, block_rows),
            block_before,
        ),
    )
    local_out = local_out.reshape(rows_here, heads_here, head_dim)
    cumul_all = jnp.cumsum(log_decay, axis=0)
    through = jnp.where(seg_now[-1] == seg_before, jnp.exp(cumul_all[-1]), 0.0)
    carried_in = carried_in_scan(through, local_state, -(-MOST // rows_here))
    carried = jnp.where((seg_now == seg_before)[:, None], jnp.exp(cumul_all), 0.0)
    from_state = jnp.einsum("tn,hpn->thp", read_rows, carried_in, precision=highest)
    ssm_y = local_out + carried[:, :, None] * from_state
    final_state = local_state + through[:, None, None] * carried_in
    gated_rows = ssm_y.reshape(rows_here, inner_here) * jax.nn.silu(gate_z)
    square_part = jnp.sum(gated_rows * gated_rows, axis=1)
    gained = (gated_rows * gate_gain).astype(jnp.bfloat16)
    mix_terms = jnp.dot(gained, w_out, preferred_element_type=jnp.float32)
    with_squares = jnp.concatenate([mix_terms, jnp.tile(square_part[None], (1, tensor_size))], axis=0)
    reduced = tp_scatter(with_squares, jnp.bfloat16)
    factor = lax.rsqrt(reduced[rows_here] / (inner_here * tensor_size) + epsilon)
    mix_share = reduced[:rows_here] * factor[:, None]
    mid_here = (hidden_in.astype(jnp.float32) + mix_share).astype(jnp.bfloat16)
    mid_full = tp_gather(mid_here, 1)
    joined = jnp.concatenate([mid_full, full_embeds], axis=1)
    attn_in = rms_rows(joined, attn_gain).astype(jnp.bfloat16)
    low_sum = accumulate_rows(attn_in, full_down)
    low_rank = low_sum.astype(jnp.bfloat16)
    rank_cols = adapter_up.shape[1]
    cols_here = w_qkv.shape[2]
    heads_attn = cols_here // AHD
    projected = jnp.dot(
        attn_in, w_qkv.reshape(w_qkv.shape[0], 3 * cols_here), preferred_element_type=jnp.float32
    ).reshape(rows_here, 3, cols_here)
    projected = projected + jnp.einsum(
        "tjr,jrc->tjc",
        low_rank.reshape(rows_here, 3, rank_cols),
        adapter_up,
        preferred_element_type=jnp.float32,
    )
    places = lax.dynamic_slice_in_dim(positions_of(seg_ids), first_row, rows_here, 0)
    queries = rotate(projected[:, 0].reshape(rows_here, heads_attn, AHD), places).astype(
        jnp.bfloat16
    )
    key_rows = rotate(projected[:, 1].reshape(rows_here, heads_attn, AHD), places).astype(
        jnp.bfloat16
    )
    value_rows = projected[:, 2].astype(jnp.bfloat16)
    kv_pair = jnp.stack([key_rows.reshape(rows_here, cols_here), value_rows], axis=1)
    query_index = first_row + jnp.arange(rows_here, dtype=jnp.int32)
    inv_root = 1.0 / math.sqrt(AHD)

    def absorb(running, block_kv, first_key):
        row_top, denom_sum, weighted = running
        key_count = block_kv.shape[0]
        key_index = first_key + jnp.arange(key_count, dtype=jnp.int32)
        key_seg = lax.dynamic_slice_in_dim(seg_ids, jnp.maximum(first_key, 0), key_count, 0)
        allowed = (
            (key_seg[None, :] == seg_now[:, None])
            & (key_index[None, :] <= query_index[:, None])
            & (key_index[None, :] >= 0)
        )
        block_keys = block_kv[:, 0].reshape(key_count, heads_attn, AHD)
        block_vals = block_kv[:, 1].reshape(key_count, heads_attn, AHD)
        scores = (
            jnp.einsum("qhe,khe->hqk", queries, block_keys, preferred_element_type=jnp.float32)
            * inv_root
        )
        masked = jnp.where(allowed[None], scores, -1e30)
        new_top = jnp.maximum(row_top, jnp.max(masked, axis=-1))
        weights = jnp.where(allowed[None], jnp.exp(scores - new_top[:, :, None]), 0.0)
        shrink = jnp.exp(row_top - new_top)
        denom_sum = denom_sum * shrink + jnp.sum(weights, axis=-1)
        weighted = weighted * shrink[:, :, None] + jnp.einsum(
            "hqk,khe->hqe",
            weights.astype(jnp.bfloat16),
            block_vals,
            preferred_element_type=jnp.float32,
        )
        return (new_top, denom_sum, weighted)

    start_state = (
        jnp.full((heads_attn, rows_here), -1e30, jnp.float32),
        jnp.zeros((heads_attn, rows_here), jnp.float32),
        jnp.zeros((heads_attn, rows_here, AHD), jnp.float32),
    )
    reach_hops = min(lax.axis_size("req") - 1, -(-(MOST - 1) // rows_here))
    running = absorb(start_state, kv_pair, first_row)
    for hop_count in range(1, reach_hops + 1):
        moving = from_behind(kv_pair, "req", hop_count)
        running = absorb(running, moving, first_row - hop_count * rows_here)
    row_top, denom_sum, weighted = running
    attended = (weighted / denom_sum[:, :, None]).astype(jnp.bfloat16)
    attended = attended.transpose(1, 0, 2).reshape(rows_here, cols_here)
    attn_terms = jnp.dot(attended, w_o, preferred_element_type=jnp.float32)
    attn_share = tp_scatter(attn_terms, jnp.bfloat16)
    hidden_out = (mid_here.astype(jnp.float32) + attn_share).astype(jnp.bfloat16)
    return (hidden_out, final_state[None], kv_pair)


def solution(mesh):
    in_specs = (
        P("req", "tp"),
        P("req", "tp"),
        P(),
        P(),
        P(None, "tp"),
        P(None, "tp"),
        P("tp", None),
        P(None, "tp"),
        P("tp"),
        P("tp"),
        P(None, "tp"),
        P(),
        P("tp"),
        P("tp"),
        P("tp", None),
        P(),
        P(None, None, "tp"),
        P("tp", None),
        P(None, None, "tp"),
        P("tp", None),
    )
    out_specs = (P("req", "tp"), P("req", "tp", None, None), P("req", None, "tp"))
    return jax.shard_map(
        on_device, mesh=mesh, in_specs=in_specs, out_specs=out_specs, check_vma=False
    )
```

```python
import math

import jax
import jax.numpy as jnp
from jax import lax
from jax.sharding import PartitionSpec as P

AHD = 128


highest = lax.Precision.HIGHEST
epsilon = 1e-05


def from_behind(block, axis, distance):
    devices = range(lax.axis_size(axis))
    route = [(i - distance, i) for i in devices if i - distance in devices]
    return lax.ppermute(block, axis, route)


def carried_in_2(value, axis, join, neutral):
    count, mine = (lax.axis_size(axis), lax.axis_index(axis))
    pieces = jax.tree.map(lambda part: lax.all_gather(part, axis), value)
    so_far = jax.tree.map(
        lambda part, zero: jnp.full_like(part, 0) + jnp.asarray(zero, part.dtype), value, neutral
    )

    def lap(position, so_far):
        longer = join(so_far, jax.tree.map(lambda part: part[position], pieces))
        return jax.tree.map(lambda new, old: jnp.where(position < mine, new, old), longer, so_far)

    return lax.fori_loop(0, count - 1, lap, so_far)


MOST = 2048


def shifted(block, axis, distance):
    count = lax.axis_size(axis)
    return lax.ppermute(block, axis, [(i, (i + distance) % count) for i in range(count)])


def tp_layout():
    count = lax.axis_size("tp")
    inner = 2 if count % 2 == 0 else 1
    return count, inner, count // inner


def tp_pieces(block):
    count, inner, outer = tp_layout()
    inner_rank = lax.axis_index("tp") % inner
    sources = [block]
    if inner == 2:
        sources.append(lax.ppermute(block, "tp", [(i, i ^ 1) for i in range(count)]))
    slots = [[source if step == 0 else shifted(source, "tp", -inner * step) for source in sources]
             for step in range(outer)]
    pieces = []
    for own, *other in slots:
        if inner == 2:
            pieces.append(jnp.where(inner_rank == 0, own, other[0]))
            pieces.append(jnp.where(inner_rank == 0, other[0], own))
        else:
            pieces.append(own)
    return pieces


def tp_assemble(pieces, axis):
    count, inner, outer = tp_layout()
    outer_rank = lax.axis_index("tp") // inner
    width = pieces[0].shape[axis]
    doubled = jnp.concatenate(pieces + pieces, axis=axis)
    start = ((count - inner * outer_rank) % count) * width
    return lax.dynamic_slice_in_dim(doubled, start, count * width, axis)


def tp_gather(block, axis):
    return tp_assemble(tp_pieces(block), axis)


def tp_scatter(values, send_dtype):
    count, inner, outer = tp_layout()
    rank = lax.axis_index("tp")
    outer_rank, inner_rank = rank // inner, rank % inner
    width = values.shape[1] // count
    span = inner * width
    total = lax.dynamic_slice_in_dim(values, outer_rank * span, span, 1).astype(jnp.float32)
    for step in range(1, outer):
        piece = lax.dynamic_slice_in_dim(values, ((outer_rank + step) % outer) * span, span, 1)
        total = total + shifted(piece.astype(send_dtype), "tp", inner * step).astype(jnp.float32)
    mine = lax.dynamic_slice_in_dim(total, inner_rank * width, width, 1)
    if inner == 2:
        theirs = lax.dynamic_slice_in_dim(total, (1 - inner_rank) * width, width, 1)
        swapped = lax.ppermute(theirs.astype(send_dtype), "tp", [(i, i ^ 1) for i in range(count)])
        mine = mine + swapped.astype(jnp.float32)
    return mine


def carried_in_scan(through, state, reach):
    heads = through.shape[0]

    def pack(decay, value):
        return jnp.concatenate([value.reshape(-1), decay])

    def unpack(packed):
        return (packed[-heads:], packed[:-heads].reshape(state.shape))

    rank = lax.axis_index("req")
    neutral = pack(jnp.ones_like(through), jnp.zeros_like(state))

    def earlier(packed, distance):
        return jnp.where(rank >= distance, from_behind(packed, "req", distance), neutral)

    def joined(parts):
        total = parts[0]
        for part in parts[1:]:
            total = pack(*combine_states(unpack(total), unpack(part)))
        return total

    group = min(2, reach)
    mine = pack(through, state)
    near = joined([earlier(mine, distance) for distance in range(group, 0, -1)])
    rounds = -(-reach // group)
    far = [earlier(near, group * step) for step in range(rounds - 1, 0, -1)]
    return unpack(joined(far + [near]))[1]


def rms_rows(values, gain):
    values = values.astype(jnp.float32)
    factor = lax.rsqrt(jnp.mean(values * values, axis=-1, keepdims=True) + epsilon)
    return values * factor * gain


def positions_of(seg_all):
    total_rows = seg_all.shape[0]
    indices = jnp.arange(total_rows, dtype=jnp.int32)
    begins = jnp.concatenate([jnp.ones((1,), dtype=bool), seg_all[1:] != seg_all[:-1]])
    first_index = lax.cummax(jnp.where(begins, indices, jnp.zeros_like(indices)), axis=0)
    return indices - first_index


def rotate(values, places):
    half_dim = values.shape[-1] // 2
    freqs = jnp.exp(-jnp.log(10000.0) * jnp.arange(half_dim, dtype=jnp.float32) / half_dim)
    angles = places.astype(jnp.float32)[:, None] * freqs[None, :]
    cosine = jnp.cos(angles)[:, None, :]
    sine = jnp.sin(angles)[:, None, :]
    first_half = values[..., :half_dim]
    second_half = values[..., half_dim:]
    return jnp.concatenate(
        [first_half * cosine - second_half * sine, second_half * cosine + first_half * sine],
        axis=-1,
    )


def conv_rows(extended, seg_extended, kernel, seg_now):
    kernel_len = kernel.shape[0]
    rows_out = seg_now.shape[0]
    result = jnp.zeros((rows_out, extended.shape[1]), jnp.float32)
    for offset in range(kernel_len):
        window_rows = extended[offset : offset + rows_out]
        matches = (seg_extended[offset : offset + rows_out] == seg_now)[:, None]
        result = result + jnp.where(matches, window_rows * kernel[offset][None, :], 0.0)
    return jax.nn.silu(result)


def ssd_block(
    inner, write_rows, read_rows, steps_dt, log_decay, seg_block, seg_before, state_prev, skip_gain
):
    length = inner.shape[0]
    cumul = jnp.cumsum(log_decay, axis=0)
    order = jnp.arange(length, dtype=jnp.int32)
    within = (seg_block[:, None] == seg_block[None, :]) & (order[:, None] >= order[None, :])
    spread = cumul.T[:, :, None] - cumul.T[:, None, :]
    decays = jnp.where(within[None], jnp.exp(jnp.minimum(spread, 0.0)), 0.0)
    intersection = jnp.dot(read_rows, write_rows.T, precision=highest)
    mixing = decays * intersection[None] * steps_dt.T[:, None, :]
    local_out = jnp.einsum("hts,shp->thp", mixing, inner, precision=highest)
    carried = jnp.where((seg_block == seg_before)[:, None], jnp.exp(cumul), 0.0)
    from_state = jnp.einsum("tn,hpn->thp", read_rows, state_prev, precision=highest)
    outputs = local_out + carried[:, :, None] * from_state + skip_gain[None, :, None] * inner
    tail_weight = (
        jnp.where((seg_block == seg_block[-1])[:, None], jnp.exp(cumul[-1][None, :] - cumul), 0.0)
        * steps_dt
    )
    keep_factor = jnp.where(seg_block[-1] == seg_before, jnp.exp(cumul[-1]), 0.0)
    state_next = keep_factor[:, None, None] * state_prev + jnp.einsum(
        "sh,shp,sn->hpn", tail_weight, inner, write_rows, precision=highest
    )
    return (outputs, state_next)


def accumulate_rows(left_rows, weight_rows):
    return jnp.dot(left_rows, weight_rows, preferred_element_type=jnp.float32)


def combine_states(earlier, later):
    return (earlier[0] * later[0], later[0][:, None, None] * earlier[1] + later[1])


def on_device(
    hidden_in,
    embeds,
    seg_ids,
    mamba_gain,
    w_z,
    w_x,
    w_bc,
    w_dt,
    dt_bias,
    decay_rate,
    conv_x,
    conv_bc,
    skip_gain,
    gate_gain,
    w_out,
    attn_gain,
    w_qkv,
    adapter_down,
    adapter_up,
    w_o,
):
    rows_here = hidden_in.shape[0]
    tensor_size = lax.axis_size("tp")
    req_rank = lax.axis_index("req")
    first_row = req_rank * rows_here
    paired = tp_pieces(jnp.stack([hidden_in, w_bc]))
    full_hidden = tp_assemble([piece[0] for piece in paired], 1)
    full_w_bc = tp_assemble([piece[1] for piece in paired], 0)
    normed = rms_rows(full_hidden, mamba_gain).astype(jnp.bfloat16)
    normed, embeds, adapter_down = lax.optimization_barrier((normed, embeds, adapter_down))
    full_embeds = tp_gather(embeds, 1)
    full_down = tp_gather(adapter_down, 0)
    gate_z = jnp.dot(normed, w_z, preferred_element_type=jnp.float32)
    inner_x = jnp.dot(normed, w_x, preferred_element_type=jnp.float32)
    raw_dt = jnp.dot(normed, w_dt, preferred_element_type=jnp.float32)
    state_io = accumulate_rows(normed, full_w_bc)
    mixed_in = jnp.concatenate([inner_x, state_io], axis=1)
    kernel_len = conv_x.shape[0]
    tail_rows = mixed_in[rows_here - (kernel_len - 1) :]
    prior_rows = from_behind(tail_rows, "req", 1)
    extended = jnp.concatenate([prior_rows, mixed_in], axis=0)
    seg_padded = jnp.concatenate(
        [jnp.full((kernel_len - 1,), -1, dtype=jnp.int32), seg_ids], axis=0
    )
    seg_extended = lax.dynamic_slice_in_dim(seg_padded, first_row, rows_here + kernel_len - 1, 0)
    seg_now = lax.dynamic_slice_in_dim(seg_ids, first_row, rows_here, 0)
    kernel = jnp.concatenate([conv_x, conv_bc], axis=1)
    conv_out = conv_rows(extended, seg_extended, kernel, seg_now)
    inner_here = w_z.shape[1]
    heads_here = w_dt.shape[1]
    head_dim = inner_here // heads_here
    state_dim = state_io.shape[1] // 2
    inner_c = conv_out[:, :inner_here].reshape(rows_here, heads_here, head_dim)
    write_rows = conv_out[:, inner_here : inner_here + state_dim]
    read_rows = conv_out[:, inner_here + state_dim :]
    steps_dt = jax.nn.softplus(raw_dt + dt_bias)
    log_decay = -steps_dt * decay_rate
    seg_before = jnp.where(req_rank > 0, seg_ids[jnp.maximum(first_row - 1, 0)], -1)
    seg_prior = jnp.concatenate([seg_before[None], seg_now[:-1]], axis=0)
    block_rows = math.gcd(rows_here, 256)
    count_blocks = rows_here // block_rows
    block_before = seg_prior.reshape(count_blocks, block_rows)[:, 0]

    def ssd_step(state_prev, pieces):
        blk_inner, blk_write, blk_read, blk_dt, blk_decay, blk_seg, blk_before = pieces
        outputs, state_next = ssd_block(
            blk_inner,
            blk_write,
            blk_read,
            blk_dt,
            blk_decay,
            blk_seg,
            blk_before,
            state_prev,
            skip_gain,
        )
        return (state_next, outputs)

    zero_state = jnp.zeros((heads_here, head_dim, state_dim), jnp.float32)
    local_state, local_out = lax.scan(
        ssd_step,
        zero_state,
        (
            inner_c.reshape(count_blocks, block_rows, heads_here, head_dim),
            write_rows.reshape(count_blocks, block_rows, state_dim),
            read_rows.reshape(count_blocks, block_rows, state_dim),
            steps_dt.reshape(count_blocks, block_rows, heads_here),
            log_decay.reshape(count_blocks, block_rows, heads_here),
            seg_now.reshape(count_blocks, block_rows),
            block_before,
        ),
    )
    local_out = local_out.reshape(rows_here, heads_here, head_dim)
    cumul_all = jnp.cumsum(log_decay, axis=0)
    through = jnp.where(seg_now[-1] == seg_before, jnp.exp(cumul_all[-1]), 0.0)
    carried_in = carried_in_scan(through, local_state, -(-MOST // rows_here))
    carried = jnp.where((seg_now == seg_before)[:, None], jnp.exp(cumul_all), 0.0)
    from_state = jnp.einsum("tn,hpn->thp", read_rows, carried_in, precision=highest)
    ssm_y = local_out + carried[:, :, None] * from_state
    final_state = local_state + through[:, None, None] * carried_in
    gated_rows = ssm_y.reshape(rows_here, inner_here) * jax.nn.silu(gate_z)
    square_part = jnp.sum(gated_rows * gated_rows, axis=1)
    gained = (gated_rows * gate_gain).astype(jnp.bfloat16)
    mix_terms = jnp.dot(gained, w_out, preferred_element_type=jnp.float32)
    with_squares = jnp.concatenate([mix_terms, jnp.tile(square_part[None], (1, tensor_size))], axis=0)
    reduced = tp_scatter(with_squares, jnp.bfloat16)
    factor = lax.rsqrt(reduced[rows_here] / (inner_here * tensor_size) + epsilon)
    mix_share = reduced[:rows_here] * factor[:, None]
    mid_here = (hidden_in.astype(jnp.float32) + mix_share).astype(jnp.bfloat16)
    mid_full = tp_gather(mid_here, 1)
    joined = jnp.concatenate([mid_full, full_embeds], axis=1)
    attn_in = rms_rows(joined, attn_gain).astype(jnp.bfloat16)
    low_sum = accumulate_rows(attn_in, full_down)
    low_rank = low_sum.astype(jnp.bfloat16)
    rank_cols = adapter_up.shape[1]
    cols_here = w_qkv.shape[2]
    heads_attn = cols_here // AHD
    projected = jnp.dot(
        attn_in, w_qkv.reshape(w_qkv.shape[0], 3 * cols_here), preferred_element_type=jnp.float32
    ).reshape(rows_here, 3, cols_here)
    projected = projected + jnp.einsum(
        "tjr,jrc->tjc",
        low_rank.reshape(rows_here, 3, rank_cols),
        adapter_up,
        preferred_element_type=jnp.float32,
    )
    places = lax.dynamic_slice_in_dim(positions_of(seg_ids), first_row, rows_here, 0)
    queries = rotate(projected[:, 0].reshape(rows_here, heads_attn, AHD), places).astype(
        jnp.bfloat16
    )
    key_rows = rotate(projected[:, 1].reshape(rows_here, heads_attn, AHD), places).astype(
        jnp.bfloat16
    )
    value_rows = projected[:, 2].astype(jnp.bfloat16)
    kv_pair = jnp.stack([key_rows.reshape(rows_here, cols_here), value_rows], axis=1)
    query_index = first_row + jnp.arange(rows_here, dtype=jnp.int32)
    inv_root = 1.0 / math.sqrt(AHD)

    def absorb(running, block_kv, first_key):
        row_top, denom_sum, weighted = running
        key_count = block_kv.shape[0]
        key_index = first_key + jnp.arange(key_count, dtype=jnp.int32)
        key_seg = lax.dynamic_slice_in_dim(seg_ids, jnp.maximum(first_key, 0), key_count, 0)
        allowed = (
            (key_seg[None, :] == seg_now[:, None])
            & (key_index[None, :] <= query_index[:, None])
            & (key_index[None, :] >= 0)
        )
        block_keys = block_kv[:, 0].reshape(key_count, heads_attn, AHD)
        block_vals = block_kv[:, 1].reshape(key_count, heads_attn, AHD)
        scores = (
            jnp.einsum("qhe,khe->hqk", queries, block_keys, preferred_element_type=jnp.float32)
            * inv_root
        )
        masked = jnp.where(allowed[None], scores, -1e30)
        new_top = jnp.maximum(row_top, jnp.max(masked, axis=-1))
        weights = jnp.where(allowed[None], jnp.exp(scores - new_top[:, :, None]), 0.0)
        shrink = jnp.exp(row_top - new_top)
        denom_sum = denom_sum * shrink + jnp.sum(weights, axis=-1)
        weighted = weighted * shrink[:, :, None] + jnp.einsum(
            "hqk,khe->hqe",
            weights.astype(jnp.bfloat16),
            block_vals,
            preferred_element_type=jnp.float32,
        )
        return (new_top, denom_sum, weighted)

    start_state = (
        jnp.full((heads_attn, rows_here), -1e30, jnp.float32),
        jnp.zeros((heads_attn, rows_here), jnp.float32),
        jnp.zeros((heads_attn, rows_here, AHD), jnp.float32),
    )
    reach_hops = min(lax.axis_size("req") - 1, -(-(MOST - 1) // rows_here))
    running = absorb(start_state, kv_pair, first_row)
    held = [kv_pair]
    while len(held) <= reach_hops:
        step = len(held)
        count = min(step, reach_hops + 1 - step)
        moved = from_behind(jnp.stack(held[:count]), "req", step)
        for offset in range(count):
            held.append(moved[offset])
            hop_count = step + offset
            running = absorb(running, moved[offset], first_row - hop_count * rows_here)
    row_top, denom_sum, weighted = running
    attended = (weighted / denom_sum[:, :, None]).astype(jnp.bfloat16)
    attended = attended.transpose(1, 0, 2).reshape(rows_here, cols_here)
    attn_terms = jnp.dot(attended, w_o, preferred_element_type=jnp.float32)
    attn_share = tp_scatter(attn_terms, jnp.bfloat16)
    hidden_out = (mid_here.astype(jnp.float32) + attn_share).astype(jnp.bfloat16)
    return (hidden_out, final_state[None], kv_pair)


def solution(mesh):
    in_specs = (
        P("req", "tp"),
        P("req", "tp"),
        P(),
        P(),
        P(None, "tp"),
        P(None, "tp"),
        P("tp", None),
        P(None, "tp"),
        P("tp"),
        P("tp"),
        P(None, "tp"),
        P(),
        P("tp"),
        P("tp"),
        P("tp", None),
        P(),
        P(None, None, "tp"),
        P("tp", None),
        P(None, None, "tp"),
        P("tp", None),
    )
    out_specs = (P("req", "tp"), P("req", "tp", None, None), P("req", None, "tp"))
    return jax.shard_map(
        on_device, mesh=mesh, in_specs=in_specs, out_specs=out_specs, check_vma=False
    )
```

```python
import math

import jax
import jax.numpy as jnp
from jax import lax
from jax.sharding import PartitionSpec as P

AHD = 128


highest = lax.Precision.HIGHEST
epsilon = 1e-05


def from_behind(block, axis, distance):
    devices = range(lax.axis_size(axis))
    route = [(i - distance, i) for i in devices if i - distance in devices]
    return lax.ppermute(block, axis, route)


def carried_in_2(value, axis, join, neutral):
    count, mine = (lax.axis_size(axis), lax.axis_index(axis))
    pieces = jax.tree.map(lambda part: lax.all_gather(part, axis), value)
    so_far = jax.tree.map(
        lambda part, zero: jnp.full_like(part, 0) + jnp.asarray(zero, part.dtype), value, neutral
    )

    def lap(position, so_far):
        longer = join(so_far, jax.tree.map(lambda part: part[position], pieces))
        return jax.tree.map(lambda new, old: jnp.where(position < mine, new, old), longer, so_far)

    return lax.fori_loop(0, count - 1, lap, so_far)


MOST = 2048


def shifted(block, axis, distance):
    count = lax.axis_size(axis)
    return lax.ppermute(block, axis, [(i, (i + distance) % count) for i in range(count)])


def tp_layout():
    count = lax.axis_size("tp")
    inner = 2 if count % 2 == 0 else 1
    return count, inner, count // inner


def tp_pieces(block):
    count, inner, outer = tp_layout()
    inner_rank = lax.axis_index("tp") % inner
    sources = [block]
    if inner == 2:
        sources.append(lax.ppermute(block, "tp", [(i, i ^ 1) for i in range(count)]))
    slots = [[source if step == 0 else shifted(source, "tp", -inner * step) for source in sources]
             for step in range(outer)]
    pieces = []
    for own, *other in slots:
        if inner == 2:
            pieces.append(jnp.where(inner_rank == 0, own, other[0]))
            pieces.append(jnp.where(inner_rank == 0, other[0], own))
        else:
            pieces.append(own)
    return pieces


def tp_assemble(pieces, axis):
    count, inner, outer = tp_layout()
    outer_rank = lax.axis_index("tp") // inner
    width = pieces[0].shape[axis]
    doubled = jnp.concatenate(pieces + pieces, axis=axis)
    start = ((count - inner * outer_rank) % count) * width
    return lax.dynamic_slice_in_dim(doubled, start, count * width, axis)


def tp_gather(block, axis):
    return tp_assemble(tp_pieces(block), axis)


def tp_scatter(values, send_dtype):
    count, inner, outer = tp_layout()
    rank = lax.axis_index("tp")
    outer_rank, inner_rank = rank // inner, rank % inner
    width = values.shape[1] // count
    span = inner * width
    total = lax.dynamic_slice_in_dim(values, outer_rank * span, span, 1).astype(jnp.float32)
    for step in range(1, outer):
        piece = lax.dynamic_slice_in_dim(values, ((outer_rank + step) % outer) * span, span, 1)
        total = total + shifted(piece.astype(send_dtype), "tp", inner * step).astype(jnp.float32)
    mine = lax.dynamic_slice_in_dim(total, inner_rank * width, width, 1)
    if inner == 2:
        theirs = lax.dynamic_slice_in_dim(total, (1 - inner_rank) * width, width, 1)
        swapped = lax.ppermute(theirs.astype(send_dtype), "tp", [(i, i ^ 1) for i in range(count)])
        mine = mine + swapped.astype(jnp.float32)
    return mine


def carried_in_scan(through, state, reach):
    heads = through.shape[0]

    def pack(decay, value):
        return jnp.concatenate([value.reshape(-1), decay])

    def unpack(packed):
        return (packed[-heads:], packed[:-heads].reshape(state.shape))

    rank = lax.axis_index("req")
    neutral = pack(jnp.ones_like(through), jnp.zeros_like(state))

    def earlier(packed, distance):
        return jnp.where(rank >= distance, from_behind(packed, "req", distance), neutral)

    def joined(parts):
        total = parts[0]
        for part in parts[1:]:
            total = pack(*combine_states(unpack(total), unpack(part)))
        return total

    group = min(2, reach)
    mine = pack(through, state)
    near = joined([earlier(mine, distance) for distance in range(group, 0, -1)])
    rounds = -(-reach // group)
    far = [earlier(near, group * step) for step in range(rounds - 1, 0, -1)]
    return unpack(joined(far + [near]))[1]


def rms_rows(values, gain):
    values = values.astype(jnp.float32)
    factor = lax.rsqrt(jnp.mean(values * values, axis=-1, keepdims=True) + epsilon)
    return values * factor * gain


def positions_of(seg_all):
    total_rows = seg_all.shape[0]
    indices = jnp.arange(total_rows, dtype=jnp.int32)
    begins = jnp.concatenate([jnp.ones((1,), dtype=bool), seg_all[1:] != seg_all[:-1]])
    first_index = lax.cummax(jnp.where(begins, indices, jnp.zeros_like(indices)), axis=0)
    return indices - first_index


def rotate(values, places):
    half_dim = values.shape[-1] // 2
    freqs = jnp.exp(-jnp.log(10000.0) * jnp.arange(half_dim, dtype=jnp.float32) / half_dim)
    angles = places.astype(jnp.float32)[:, None] * freqs[None, :]
    cosine = jnp.cos(angles)[:, None, :]
    sine = jnp.sin(angles)[:, None, :]
    first_half = values[..., :half_dim]
    second_half = values[..., half_dim:]
    return jnp.concatenate(
        [first_half * cosine - second_half * sine, second_half * cosine + first_half * sine],
        axis=-1,
    )


def conv_rows(extended, seg_extended, kernel, seg_now):
    kernel_len = kernel.shape[0]
    rows_out = seg_now.shape[0]
    result = jnp.zeros((rows_out, extended.shape[1]), jnp.float32)
    for offset in range(kernel_len):
        window_rows = extended[offset : offset + rows_out]
        matches = (seg_extended[offset : offset + rows_out] == seg_now)[:, None]
        result = result + jnp.where(matches, window_rows * kernel[offset][None, :], 0.0)
    return jax.nn.silu(result)


def ssd_block(
    inner, write_rows, read_rows, steps_dt, log_decay, seg_block, seg_before, state_prev, skip_gain
):
    length = inner.shape[0]
    cumul = jnp.cumsum(log_decay, axis=0)
    order = jnp.arange(length, dtype=jnp.int32)
    within = (seg_block[:, None] == seg_block[None, :]) & (order[:, None] >= order[None, :])
    spread = cumul.T[:, :, None] - cumul.T[:, None, :]
    decays = jnp.where(within[None], jnp.exp(jnp.minimum(spread, 0.0)), 0.0)
    intersection = jnp.dot(read_rows, write_rows.T, precision=highest)
    mixing = decays * intersection[None] * steps_dt.T[:, None, :]
    local_out = jnp.einsum("hts,shp->thp", mixing, inner, precision=highest)
    carried = jnp.where((seg_block == seg_before)[:, None], jnp.exp(cumul), 0.0)
    from_state = jnp.einsum("tn,hpn->thp", read_rows, state_prev, precision=highest)
    outputs = local_out + carried[:, :, None] * from_state + skip_gain[None, :, None] * inner
    tail_weight = (
        jnp.where((seg_block == seg_block[-1])[:, None], jnp.exp(cumul[-1][None, :] - cumul), 0.0)
        * steps_dt
    )
    keep_factor = jnp.where(seg_block[-1] == seg_before, jnp.exp(cumul[-1]), 0.0)
    state_next = keep_factor[:, None, None] * state_prev + jnp.einsum(
        "sh,shp,sn->hpn", tail_weight, inner, write_rows, precision=highest
    )
    return (outputs, state_next)


def accumulate_rows(left_rows, weight_rows):
    return jnp.dot(left_rows, weight_rows, preferred_element_type=jnp.float32)


def combine_states(earlier, later):
    return (earlier[0] * later[0], later[0][:, None, None] * earlier[1] + later[1])


def on_device(
    hidden_in,
    embeds,
    seg_ids,
    mamba_gain,
    w_z,
    w_x,
    w_bc,
    w_dt,
    dt_bias,
    decay_rate,
    conv_x,
    conv_bc,
    skip_gain,
    gate_gain,
    w_out,
    attn_gain,
    w_qkv,
    adapter_down,
    adapter_up,
    w_o,
):
    rows_here = hidden_in.shape[0]
    tensor_size = lax.axis_size("tp")
    req_rank = lax.axis_index("req")
    first_row = req_rank * rows_here
    paired = tp_pieces(jnp.stack([hidden_in, w_bc]))
    full_hidden = tp_assemble([piece[0] for piece in paired], 1)
    full_w_bc = tp_assemble([piece[1] for piece in paired], 0)
    normed = rms_rows(full_hidden, mamba_gain).astype(jnp.bfloat16)
    normed, embeds, adapter_down = lax.optimization_barrier((normed, embeds, adapter_down))
    full_embeds = tp_gather(embeds, 1)
    full_down = tp_gather(adapter_down, 0)
    gate_z = jnp.dot(normed, w_z, preferred_element_type=jnp.float32)
    inner_x = jnp.dot(normed, w_x, preferred_element_type=jnp.float32)
    raw_dt = jnp.dot(normed, w_dt, preferred_element_type=jnp.float32)
    state_io = accumulate_rows(normed, full_w_bc)
    mixed_in = jnp.concatenate([inner_x, state_io], axis=1)
    kernel_len = conv_x.shape[0]
    tail_rows = mixed_in[rows_here - (kernel_len - 1) :]
    prior_rows = from_behind(tail_rows, "req", 1)
    extended = jnp.concatenate([prior_rows, mixed_in], axis=0)
    seg_padded = jnp.concatenate(
        [jnp.full((kernel_len - 1,), -1, dtype=jnp.int32), seg_ids], axis=0
    )
    seg_extended = lax.dynamic_slice_in_dim(seg_padded, first_row, rows_here + kernel_len - 1, 0)
    seg_now = lax.dynamic_slice_in_dim(seg_ids, first_row, rows_here, 0)
    kernel = jnp.concatenate([conv_x, conv_bc], axis=1)
    conv_out = conv_rows(extended, seg_extended, kernel, seg_now)
    inner_here = w_z.shape[1]
    heads_here = w_dt.shape[1]
    head_dim = inner_here // heads_here
    state_dim = state_io.shape[1] // 2
    inner_c = conv_out[:, :inner_here].reshape(rows_here, heads_here, head_dim)
    write_rows = conv_out[:, inner_here : inner_here + state_dim]
    read_rows = conv_out[:, inner_here + state_dim :]
    steps_dt = jax.nn.softplus(raw_dt + dt_bias)
    log_decay = -steps_dt * decay_rate
    seg_before = jnp.where(req_rank > 0, seg_ids[jnp.maximum(first_row - 1, 0)], -1)
    seg_prior = jnp.concatenate([seg_before[None], seg_now[:-1]], axis=0)
    block_rows = math.gcd(rows_here, 256)
    count_blocks = rows_here // block_rows
    block_before = seg_prior.reshape(count_blocks, block_rows)[:, 0]

    def ssd_step(state_prev, pieces):
        blk_inner, blk_write, blk_read, blk_dt, blk_decay, blk_seg, blk_before = pieces
        outputs, state_next = ssd_block(
            blk_inner,
            blk_write,
            blk_read,
            blk_dt,
            blk_decay,
            blk_seg,
            blk_before,
            state_prev,
            skip_gain,
        )
        return (state_next, outputs)

    zero_state = jnp.zeros((heads_here, head_dim, state_dim), jnp.float32)
    local_state, local_out = lax.scan(
        ssd_step,
        zero_state,
        (
            inner_c.reshape(count_blocks, block_rows, heads_here, head_dim),
            write_rows.reshape(count_blocks, block_rows, state_dim),
            read_rows.reshape(count_blocks, block_rows, state_dim),
            steps_dt.reshape(count_blocks, block_rows, heads_here),
            log_decay.reshape(count_blocks, block_rows, heads_here),
            seg_now.reshape(count_blocks, block_rows),
            block_before,
        ),
    )
    local_out = local_out.reshape(rows_here, heads_here, head_dim)
    cumul_all = jnp.cumsum(log_decay, axis=0)
    through = jnp.where(seg_now[-1] == seg_before, jnp.exp(cumul_all[-1]), 0.0)
    carried_in = carried_in_scan(through, local_state, -(-MOST // rows_here))
    carried = jnp.where((seg_now == seg_before)[:, None], jnp.exp(cumul_all), 0.0)
    from_state = jnp.einsum("tn,hpn->thp", read_rows, carried_in, precision=highest)
    ssm_y = local_out + carried[:, :, None] * from_state
    final_state = local_state + through[:, None, None] * carried_in
    gated_rows = ssm_y.reshape(rows_here, inner_here) * jax.nn.silu(gate_z)
    square_part = jnp.sum(gated_rows * gated_rows, axis=1)
    gained = (gated_rows * gate_gain).astype(jnp.bfloat16)
    mix_terms = jnp.dot(gained, w_out, preferred_element_type=jnp.float32)
    with_squares = jnp.concatenate([mix_terms, jnp.tile(square_part[None], (1, tensor_size))], axis=0)
    reduced = tp_scatter(with_squares, jnp.bfloat16)
    factor = lax.rsqrt(reduced[rows_here] / (inner_here * tensor_size) + epsilon)
    mix_share = reduced[:rows_here] * factor[:, None]
    mid_here = (hidden_in.astype(jnp.float32) + mix_share).astype(jnp.bfloat16)
    mid_full = tp_gather(mid_here, 1)
    joined = jnp.concatenate([mid_full, full_embeds], axis=1)
    attn_in = rms_rows(joined, attn_gain).astype(jnp.bfloat16)
    low_sum = accumulate_rows(attn_in, full_down)
    low_rank = low_sum.astype(jnp.bfloat16)
    rank_cols = adapter_up.shape[1]
    cols_here = w_qkv.shape[2]
    heads_attn = cols_here // AHD
    projected = jnp.dot(
        attn_in, w_qkv.reshape(w_qkv.shape[0], 3 * cols_here), preferred_element_type=jnp.float32
    ).reshape(rows_here, 3, cols_here)
    projected = projected + jnp.einsum(
        "tjr,jrc->tjc",
        low_rank.reshape(rows_here, 3, rank_cols),
        adapter_up,
        preferred_element_type=jnp.float32,
    )
    places = lax.dynamic_slice_in_dim(positions_of(seg_ids), first_row, rows_here, 0)
    queries = rotate(projected[:, 0].reshape(rows_here, heads_attn, AHD), places).astype(
        jnp.bfloat16
    )
    key_rows = rotate(projected[:, 1].reshape(rows_here, heads_attn, AHD), places).astype(
        jnp.bfloat16
    )
    value_rows = projected[:, 2].astype(jnp.bfloat16)
    kv_pair = jnp.stack([key_rows.reshape(rows_here, cols_here), value_rows], axis=1)
    query_index = first_row + jnp.arange(rows_here, dtype=jnp.int32)
    inv_root = 1.0 / math.sqrt(AHD)

    def absorb(running, block_kv, first_key):
        row_top, denom_sum, weighted = running
        key_count = block_kv.shape[0]
        key_index = first_key + jnp.arange(key_count, dtype=jnp.int32)
        key_seg = lax.dynamic_slice_in_dim(seg_ids, jnp.maximum(first_key, 0), key_count, 0)
        allowed = (
            (key_seg[None, :] == seg_now[:, None])
            & (key_index[None, :] <= query_index[:, None])
            & (key_index[None, :] >= 0)
        )
        block_keys = block_kv[:, 0].reshape(key_count, heads_attn, AHD)
        block_vals = block_kv[:, 1].reshape(key_count, heads_attn, AHD)
        scores = (
            jnp.einsum("qhe,khe->hqk", queries, block_keys, preferred_element_type=jnp.float32)
            * inv_root
        )
        masked = jnp.where(allowed[None], scores, -1e30)
        new_top = jnp.maximum(row_top, jnp.max(masked, axis=-1))
        weights = jnp.where(allowed[None], jnp.exp(scores - new_top[:, :, None]), 0.0)
        shrink = jnp.exp(row_top - new_top)
        denom_sum = denom_sum * shrink + jnp.sum(weights, axis=-1)
        weighted = weighted * shrink[:, :, None] + jnp.einsum(
            "hqk,khe->hqe",
            weights.astype(jnp.bfloat16),
            block_vals,
            preferred_element_type=jnp.float32,
        )
        return (new_top, denom_sum, weighted)

    start_state = (
        jnp.full((heads_attn, rows_here), -1e30, jnp.float32),
        jnp.zeros((heads_attn, rows_here), jnp.float32),
        jnp.zeros((heads_attn, rows_here, AHD), jnp.float32),
    )
    reach_hops = min(lax.axis_size("req") - 1, -(-(MOST - 1) // rows_here))
    running = absorb(start_state, kv_pair, first_row)

    def hop(hop_count, carry):
        moving, running = carry
        moving = from_behind(moving, "req", 1)
        return (moving, absorb(running, moving, first_row - hop_count * rows_here))

    _, running = lax.fori_loop(1, reach_hops + 1, hop, (kv_pair, running))
    row_top, denom_sum, weighted = running
    attended = (weighted / denom_sum[:, :, None]).astype(jnp.bfloat16)
    attended = attended.transpose(1, 0, 2).reshape(rows_here, cols_here)
    attn_terms = jnp.dot(attended, w_o, preferred_element_type=jnp.float32)
    attn_share = tp_scatter(attn_terms, jnp.bfloat16)
    hidden_out = (mid_here.astype(jnp.float32) + attn_share).astype(jnp.bfloat16)
    return (hidden_out, final_state[None], kv_pair)


def solution(mesh):
    in_specs = (
        P("req", "tp"),
        P("req", "tp"),
        P(),
        P(),
        P(None, "tp"),
        P(None, "tp"),
        P("tp", None),
        P(None, "tp"),
        P("tp"),
        P("tp"),
        P(None, "tp"),
        P(),
        P("tp"),
        P("tp"),
        P("tp", None),
        P(),
        P(None, None, "tp"),
        P("tp", None),
        P(None, None, "tp"),
        P("tp", None),
    )
    out_specs = (P("req", "tp"), P("req", "tp", None, None), P("req", None, "tp"))
    return jax.shard_map(
        on_device, mesh=mesh, in_specs=in_specs, out_specs=out_specs, check_vma=False
    )
```

```python
import math

import jax
import jax.numpy as jnp
from jax import lax
from jax.sharding import PartitionSpec as P

AHD = 128


highest = lax.Precision.HIGHEST
epsilon = 1e-05


def from_behind(block, axis, distance):
    devices = range(lax.axis_size(axis))
    route = [(i - distance, i) for i in devices if i - distance in devices]
    return lax.ppermute(block, axis, route)


def carried_in_2(value, axis, join, neutral):
    count, mine = (lax.axis_size(axis), lax.axis_index(axis))
    pieces = jax.tree.map(lambda part: lax.all_gather(part, axis), value)
    so_far = jax.tree.map(
        lambda part, zero: jnp.full_like(part, 0) + jnp.asarray(zero, part.dtype), value, neutral
    )

    def lap(position, so_far):
        longer = join(so_far, jax.tree.map(lambda part: part[position], pieces))
        return jax.tree.map(lambda new, old: jnp.where(position < mine, new, old), longer, so_far)

    return lax.fori_loop(0, count - 1, lap, so_far)


MOST = 2048


def shifted(block, axis, distance):
    count = lax.axis_size(axis)
    return lax.ppermute(block, axis, [(i, (i + distance) % count) for i in range(count)])


def tp_layout():
    count = lax.axis_size("tp")
    inner = 2 if count % 2 == 0 else 1
    return count, inner, count // inner


def tp_pieces(block, partner=None):
    count, inner, outer = tp_layout()
    inner_rank = lax.axis_index("tp") % inner
    sources = [block]
    if inner == 2:
        if partner is None:
            partner = lax.ppermute(block, "tp", [(i, i ^ 1) for i in range(count)])
        sources.append(partner)
    slots = [[source if step == 0 else shifted(source, "tp", -inner * step) for source in sources]
             for step in range(outer)]
    pieces = []
    for own, *other in slots:
        if inner == 2:
            pieces.append(jnp.where(inner_rank == 0, own, other[0]))
            pieces.append(jnp.where(inner_rank == 0, other[0], own))
        else:
            pieces.append(own)
    return pieces


def near_partner(block, replicated):
    count, inner, _ = tp_layout()
    across = lax.ppermute(block, "tp", [(i, i ^ 1) for i in range(count)])
    rows = lax.axis_size("req")
    if inner != 2 or rows % 8 != 0:
        return jnp.stack([across, lax.ppermute(replicated, "tp", [(i, i ^ 1) for i in range(count)])])
    pairs = []
    for row in range(rows):
        outer_row, lane, core = (row // 8, (row // 2) % 4, row % 2)
        row_to = outer_row * 8 + ((lane + 2) % 4) * 2 + core
        for col in range(count):
            pairs.append((row * count + col, row_to * count + (col ^ 1)))
    fetched = lax.ppermute(replicated, ("req", "tp"), pairs)
    return jnp.stack([across, fetched])


def tp_assemble(pieces, axis):
    count, inner, outer = tp_layout()
    outer_rank = lax.axis_index("tp") // inner
    width = pieces[0].shape[axis]
    doubled = jnp.concatenate(pieces + pieces, axis=axis)
    start = ((count - inner * outer_rank) % count) * width
    return lax.dynamic_slice_in_dim(doubled, start, count * width, axis)


def tp_gather(block, axis):
    return tp_assemble(tp_pieces(block), axis)


def tp_scatter(values, send_dtype):
    count, inner, outer = tp_layout()
    rank = lax.axis_index("tp")
    outer_rank, inner_rank = rank // inner, rank % inner
    width = values.shape[1] // count
    span = inner * width
    total = lax.dynamic_slice_in_dim(values, outer_rank * span, span, 1).astype(jnp.float32)
    for step in range(1, outer):
        piece = lax.dynamic_slice_in_dim(values, ((outer_rank + step) % outer) * span, span, 1)
        total = total + shifted(piece.astype(send_dtype), "tp", inner * step).astype(jnp.float32)
    mine = lax.dynamic_slice_in_dim(total, inner_rank * width, width, 1)
    if inner == 2:
        theirs = lax.dynamic_slice_in_dim(total, (1 - inner_rank) * width, width, 1)
        swapped = lax.ppermute(theirs.astype(send_dtype), "tp", [(i, i ^ 1) for i in range(count)])
        mine = mine + swapped.astype(jnp.float32)
    return mine


def carried_in_scan(through, state, reach):
    heads = through.shape[0]

    def pack(decay, value):
        return jnp.concatenate([value.reshape(-1), decay])

    def unpack(packed):
        return (packed[-heads:], packed[:-heads].reshape(state.shape))

    rank = lax.axis_index("req")
    neutral = pack(jnp.ones_like(through), jnp.zeros_like(state))

    def earlier(packed, distance):
        return jnp.where(rank >= distance, from_behind(packed, "req", distance), neutral)

    def joined(parts):
        total = parts[0]
        for part in parts[1:]:
            total = pack(*combine_states(unpack(total), unpack(part)))
        return total

    group = min(2, reach)
    mine = pack(through, state)
    near = joined([earlier(mine, distance) for distance in range(group, 0, -1)])
    rounds = -(-reach // group)
    far = [earlier(near, group * step) for step in range(rounds - 1, 0, -1)]
    return unpack(joined(far + [near]))[1]


def rms_rows(values, gain):
    values = values.astype(jnp.float32)
    factor = lax.rsqrt(jnp.mean(values * values, axis=-1, keepdims=True) + epsilon)
    return values * factor * gain


def positions_of(seg_all):
    total_rows = seg_all.shape[0]
    indices = jnp.arange(total_rows, dtype=jnp.int32)
    begins = jnp.concatenate([jnp.ones((1,), dtype=bool), seg_all[1:] != seg_all[:-1]])
    first_index = lax.cummax(jnp.where(begins, indices, jnp.zeros_like(indices)), axis=0)
    return indices - first_index


def rotate(values, places):
    half_dim = values.shape[-1] // 2
    freqs = jnp.exp(-jnp.log(10000.0) * jnp.arange(half_dim, dtype=jnp.float32) / half_dim)
    angles = places.astype(jnp.float32)[:, None] * freqs[None, :]
    cosine = jnp.cos(angles)[:, None, :]
    sine = jnp.sin(angles)[:, None, :]
    first_half = values[..., :half_dim]
    second_half = values[..., half_dim:]
    return jnp.concatenate(
        [first_half * cosine - second_half * sine, second_half * cosine + first_half * sine],
        axis=-1,
    )


def conv_rows(extended, seg_extended, kernel, seg_now):
    kernel_len = kernel.shape[0]
    rows_out = seg_now.shape[0]
    result = jnp.zeros((rows_out, extended.shape[1]), jnp.float32)
    for offset in range(kernel_len):
        window_rows = extended[offset : offset + rows_out]
        matches = (seg_extended[offset : offset + rows_out] == seg_now)[:, None]
        result = result + jnp.where(matches, window_rows * kernel[offset][None, :], 0.0)
    return jax.nn.silu(result)


def ssd_block(
    inner, write_rows, read_rows, steps_dt, log_decay, seg_block, seg_before, state_prev, skip_gain
):
    length = inner.shape[0]
    cumul = jnp.cumsum(log_decay, axis=0)
    order = jnp.arange(length, dtype=jnp.int32)
    within = (seg_block[:, None] == seg_block[None, :]) & (order[:, None] >= order[None, :])
    spread = cumul.T[:, :, None] - cumul.T[:, None, :]
    decays = jnp.where(within[None], jnp.exp(jnp.minimum(spread, 0.0)), 0.0)
    intersection = jnp.dot(read_rows, write_rows.T, precision=highest)
    mixing = decays * intersection[None] * steps_dt.T[:, None, :]
    local_out = jnp.einsum("hts,shp->thp", mixing, inner, precision=highest)
    carried = jnp.where((seg_block == seg_before)[:, None], jnp.exp(cumul), 0.0)
    from_state = jnp.einsum("tn,hpn->thp", read_rows, state_prev, precision=highest)
    outputs = local_out + carried[:, :, None] * from_state + skip_gain[None, :, None] * inner
    tail_weight = (
        jnp.where((seg_block == seg_block[-1])[:, None], jnp.exp(cumul[-1][None, :] - cumul), 0.0)
        * steps_dt
    )
    keep_factor = jnp.where(seg_block[-1] == seg_before, jnp.exp(cumul[-1]), 0.0)
    state_next = keep_factor[:, None, None] * state_prev + jnp.einsum(
        "sh,shp,sn->hpn", tail_weight, inner, write_rows, precision=highest
    )
    return (outputs, state_next)


def accumulate_rows(left_rows, weight_rows):
    return jnp.dot(left_rows, weight_rows, preferred_element_type=jnp.float32)


def combine_states(earlier, later):
    return (earlier[0] * later[0], later[0][:, None, None] * earlier[1] + later[1])


def on_device(
    hidden_in,
    embeds,
    seg_ids,
    mamba_gain,
    w_z,
    w_x,
    w_bc,
    w_dt,
    dt_bias,
    decay_rate,
    conv_x,
    conv_bc,
    skip_gain,
    gate_gain,
    w_out,
    attn_gain,
    w_qkv,
    adapter_down,
    adapter_up,
    w_o,
):
    rows_here = hidden_in.shape[0]
    tensor_size = lax.axis_size("tp")
    req_rank = lax.axis_index("req")
    first_row = req_rank * rows_here
    paired = tp_pieces(jnp.stack([hidden_in, w_bc]), near_partner(hidden_in, w_bc))
    full_hidden = tp_assemble([piece[0] for piece in paired], 1)
    full_w_bc = tp_assemble([piece[1] for piece in paired], 0)
    normed = rms_rows(full_hidden, mamba_gain).astype(jnp.bfloat16)
    normed, embeds, adapter_down = lax.optimization_barrier((normed, embeds, adapter_down))
    full_embeds = tp_gather(embeds, 1)
    full_down = tp_gather(adapter_down, 0)
    gate_z = jnp.dot(normed, w_z, preferred_element_type=jnp.float32)
    inner_x = jnp.dot(normed, w_x, preferred_element_type=jnp.float32)
    raw_dt = jnp.dot(normed, w_dt, preferred_element_type=jnp.float32)
    state_io = accumulate_rows(normed, full_w_bc)
    mixed_in = jnp.concatenate([inner_x, state_io], axis=1)
    kernel_len = conv_x.shape[0]
    tail_rows = mixed_in[rows_here - (kernel_len - 1) :]
    prior_rows = from_behind(tail_rows, "req", 1)
    extended = jnp.concatenate([prior_rows, mixed_in], axis=0)
    seg_padded = jnp.concatenate(
        [jnp.full((kernel_len - 1,), -1, dtype=jnp.int32), seg_ids], axis=0
    )
    seg_extended = lax.dynamic_slice_in_dim(seg_padded, first_row, rows_here + kernel_len - 1, 0)
    seg_now = lax.dynamic_slice_in_dim(seg_ids, first_row, rows_here, 0)
    kernel = jnp.concatenate([conv_x, conv_bc], axis=1)
    conv_out = conv_rows(extended, seg_extended, kernel, seg_now)
    inner_here = w_z.shape[1]
    heads_here = w_dt.shape[1]
    head_dim = inner_here // heads_here
    state_dim = state_io.shape[1] // 2
    inner_c = conv_out[:, :inner_here].reshape(rows_here, heads_here, head_dim)
    write_rows = conv_out[:, inner_here : inner_here + state_dim]
    read_rows = conv_out[:, inner_here + state_dim :]
    steps_dt = jax.nn.softplus(raw_dt + dt_bias)
    log_decay = -steps_dt * decay_rate
    seg_before = jnp.where(req_rank > 0, seg_ids[jnp.maximum(first_row - 1, 0)], -1)
    seg_prior = jnp.concatenate([seg_before[None], seg_now[:-1]], axis=0)
    block_rows = math.gcd(rows_here, 256)
    count_blocks = rows_here // block_rows
    block_before = seg_prior.reshape(count_blocks, block_rows)[:, 0]

    def ssd_step(state_prev, pieces):
        blk_inner, blk_write, blk_read, blk_dt, blk_decay, blk_seg, blk_before = pieces
        outputs, state_next = ssd_block(
            blk_inner,
            blk_write,
            blk_read,
            blk_dt,
            blk_decay,
            blk_seg,
            blk_before,
            state_prev,
            skip_gain,
        )
        return (state_next, outputs)

    zero_state = jnp.zeros((heads_here, head_dim, state_dim), jnp.float32)
    local_state, local_out = lax.scan(
        ssd_step,
        zero_state,
        (
            inner_c.reshape(count_blocks, block_rows, heads_here, head_dim),
            write_rows.reshape(count_blocks, block_rows, state_dim),
            read_rows.reshape(count_blocks, block_rows, state_dim),
            steps_dt.reshape(count_blocks, block_rows, heads_here),
            log_decay.reshape(count_blocks, block_rows, heads_here),
            seg_now.reshape(count_blocks, block_rows),
            block_before,
        ),
    )
    local_out = local_out.reshape(rows_here, heads_here, head_dim)
    cumul_all = jnp.cumsum(log_decay, axis=0)
    through = jnp.where(seg_now[-1] == seg_before, jnp.exp(cumul_all[-1]), 0.0)
    carried_in = carried_in_scan(through, local_state, -(-MOST // rows_here))
    carried = jnp.where((seg_now == seg_before)[:, None], jnp.exp(cumul_all), 0.0)
    from_state = jnp.einsum("tn,hpn->thp", read_rows, carried_in, precision=highest)
    ssm_y = local_out + carried[:, :, None] * from_state
    final_state = local_state + through[:, None, None] * carried_in
    gated_rows = ssm_y.reshape(rows_here, inner_here) * jax.nn.silu(gate_z)
    square_part = jnp.sum(gated_rows * gated_rows, axis=1)
    gained = (gated_rows * gate_gain).astype(jnp.bfloat16)
    mix_terms = jnp.dot(gained, w_out, preferred_element_type=jnp.float32)
    with_squares = jnp.concatenate([mix_terms, jnp.tile(square_part[None], (1, tensor_size))], axis=0)
    reduced = tp_scatter(with_squares, jnp.bfloat16)
    factor = lax.rsqrt(reduced[rows_here] / (inner_here * tensor_size) + epsilon)
    mix_share = reduced[:rows_here] * factor[:, None]
    mid_here = (hidden_in.astype(jnp.float32) + mix_share).astype(jnp.bfloat16)
    mid_full = tp_gather(mid_here, 1)
    joined = jnp.concatenate([mid_full, full_embeds], axis=1)
    attn_in = rms_rows(joined, attn_gain).astype(jnp.bfloat16)
    low_sum = accumulate_rows(attn_in, full_down)
    low_rank = low_sum.astype(jnp.bfloat16)
    rank_cols = adapter_up.shape[1]
    cols_here = w_qkv.shape[2]
    heads_attn = cols_here // AHD
    projected = jnp.dot(
        attn_in, w_qkv.reshape(w_qkv.shape[0], 3 * cols_here), preferred_element_type=jnp.float32
    ).reshape(rows_here, 3, cols_here)
    projected = projected + jnp.einsum(
        "tjr,jrc->tjc",
        low_rank.reshape(rows_here, 3, rank_cols),
        adapter_up,
        preferred_element_type=jnp.float32,
    )
    places = lax.dynamic_slice_in_dim(positions_of(seg_ids), first_row, rows_here, 0)
    queries = rotate(projected[:, 0].reshape(rows_here, heads_attn, AHD), places).astype(
        jnp.bfloat16
    )
    key_rows = rotate(projected[:, 1].reshape(rows_here, heads_attn, AHD), places).astype(
        jnp.bfloat16
    )
    value_rows = projected[:, 2].astype(jnp.bfloat16)
    kv_pair = jnp.stack([key_rows.reshape(rows_here, cols_here), value_rows], axis=1)
    query_index = first_row + jnp.arange(rows_here, dtype=jnp.int32)
    inv_root = 1.0 / math.sqrt(AHD)

    def absorb(running, block_kv, first_key):
        row_top, denom_sum, weighted = running
        key_count = block_kv.shape[0]
        key_index = first_key + jnp.arange(key_count, dtype=jnp.int32)
        key_seg = lax.dynamic_slice_in_dim(seg_ids, jnp.maximum(first_key, 0), key_count, 0)
        allowed = (
            (key_seg[None, :] == seg_now[:, None])
            & (key_index[None, :] <= query_index[:, None])
            & (key_index[None, :] >= 0)
        )
        block_keys = block_kv[:, 0].reshape(key_count, heads_attn, AHD)
        block_vals = block_kv[:, 1].reshape(key_count, heads_attn, AHD)
        scores = (
            jnp.einsum("qhe,khe->hqk", queries, block_keys, preferred_element_type=jnp.float32)
            * inv_root
        )
        masked = jnp.where(allowed[None], scores, -1e30)
        new_top = jnp.maximum(row_top, jnp.max(masked, axis=-1))
        weights = jnp.where(allowed[None], jnp.exp(scores - new_top[:, :, None]), 0.0)
        shrink = jnp.exp(row_top - new_top)
        denom_sum = denom_sum * shrink + jnp.sum(weights, axis=-1)
        weighted = weighted * shrink[:, :, None] + jnp.einsum(
            "hqk,khe->hqe",
            weights.astype(jnp.bfloat16),
            block_vals,
            preferred_element_type=jnp.float32,
        )
        return (new_top, denom_sum, weighted)

    start_state = (
        jnp.full((heads_attn, rows_here), -1e30, jnp.float32),
        jnp.zeros((heads_attn, rows_here), jnp.float32),
        jnp.zeros((heads_attn, rows_here, AHD), jnp.float32),
    )
    reach_hops = min(lax.axis_size("req") - 1, -(-(MOST - 1) // rows_here))
    running = absorb(start_state, kv_pair, first_row)
    for hop_count in range(1, reach_hops + 1):
        moving = from_behind(kv_pair, "req", hop_count)
        running = absorb(running, moving, first_row - hop_count * rows_here)
    row_top, denom_sum, weighted = running
    attended = (weighted / denom_sum[:, :, None]).astype(jnp.bfloat16)
    attended = attended.transpose(1, 0, 2).reshape(rows_here, cols_here)
    attn_terms = jnp.dot(attended, w_o, preferred_element_type=jnp.float32)
    attn_share = tp_scatter(attn_terms, jnp.bfloat16)
    hidden_out = (mid_here.astype(jnp.float32) + attn_share).astype(jnp.bfloat16)
    return (hidden_out, final_state[None], kv_pair)


def solution(mesh):
    in_specs = (
        P("req", "tp"),
        P("req", "tp"),
        P(),
        P(),
        P(None, "tp"),
        P(None, "tp"),
        P("tp", None),
        P(None, "tp"),
        P("tp"),
        P("tp"),
        P(None, "tp"),
        P(),
        P("tp"),
        P("tp"),
        P("tp", None),
        P(),
        P(None, None, "tp"),
        P("tp", None),
        P(None, None, "tp"),
        P("tp", None),
    )
    out_specs = (P("req", "tp"), P("req", "tp", None, None), P("req", None, "tp"))
    return jax.shard_map(
        on_device, mesh=mesh, in_specs=in_specs, out_specs=out_specs, check_vma=False
    )
```
